32 devices in a mesh: groups: 2 (over y), dom: 4 (over z), section: 4 (over x, core).
Axes of the slice: x: 2, y: 2, z: 4, core: 2. Of those that a mesh axis runs over, the one named last changes fastest.
Arguments:
- node_input: bfloat16 [4, 1024, 512], P('groups', 'dom'), parts along dimension 0, may hold values from -6 to 6
- cotangent: bfloat16 [4, 1024, 512], P('groups', 'dom'), parts along dimension 0, may hold values from -6 to 6
- w_one: bfloat16 [4, 1024, 512], P('section'), may hold values from -0.1875 to 0.1875
- w_two: bfloat16 [4, 512, 512], P('section'), may hold values from -0.25 to 0.25
- gain: float32 [4, 512], P('section'), may hold values from 0.1 to 1.9
- tile_weights: bfloat16 [40, 128, 128], P('dom'), may hold values from -0.25 to 0.25
- tile_rows: int32 [40], P('dom'), may hold values from 0 to 1, as said below
- tile_cols: int32 [40], P('dom'), may hold values from 0 to 3, as said below
- tile_count: int32 [4], P('dom'), may hold values from 4 to 10, as said below
- halo_from_left: int32 [4, 1], replicated, may hold values from 0 to 7, as said below
- halo_from_right: int32 [4, 1], replicated, may hold values from 0 to 7, as said below
Outputs:
- layer_out: bfloat16 [4, 4, 1024, 512], P('section', 'groups', 'dom'), parts along dimension 1
- input_grad: bfloat16 [4, 4, 1024, 512], P('section', 'groups', 'dom'), parts along dimension 1
- grad_w_one: float32 [4, 1024, 1024], P('section', 'dom', 'groups'), parts along dimension 2
- grad_w_two: float32 [4, 512, 1024], P('section', 'dom', 'groups'), parts along dimension 2
- grad_gain: float32 [4, 1024], P('section', ('groups', 'dom')), parts along dimension 1
The draws below stay inside these ranges and needn't reach their ends.
There are 2 independent parts, one for each index of `groups`. The reference program is written for one: setup_inputs(seed, part) draws one part's arguments, and reference() takes and returns one part's arrays. A program takes and returns all parts, laid end to end along the dimension named above; an argument that names none is the same for every part. Nothing has to cross between parts.
Inputs may be any that keep to these rules, and one draw needn't show every extreme that they name: Each partition's own blocks are tile_rows values; slots at or beyond tile_count hold valid but unused entries. `tile_cols`: index into the extended list of a partition: its 1 block from halo_from_left, its own 2 blocks, its 1 block from halo_from_right. `tile_count`: the live slots of a partition come first; some partition uses all 10 slots. `halo_from_left`: row d lists 1 distinct blocks owned by partition (d - 1) mod 4. `halo_from_right`: row d lists 1 distinct blocks owned by partition (d + 1) mod 4.
All inputs are finite; a program needn't handle non-finite values.
Results may differ from the reference program's by a relative error of at most 0.02.
Values may be sent and summed in bfloat16 or wider, within the bound.
No kernel may reach another device: no remote copies, remote signals or barrier semaphores. Data moves between devices by JAX's collectives and lax.ppermute only.
A program may use at most 128 MiB of HBM per device.

```python
import math
import jax
import jax.numpy as jnp
from jax import lax

LATENT_WIDTH = 512
BLOCK = 128
HS = 1
SAMP = 2
NB_DEV = 2
LAYERS = 4
TILES_DEV = 10
TILES = 40
NBLOCKS = 8
NODES = 1024
N_DOM = 4


def graph_tables(key):
    mixed_key = jax.random.fold_in(key, 11)
    key_count, key_full, key_rows, key_cols, key_order = jax.random.split(mixed_key, 5)
    counts = jax.random.randint(key_count, (N_DOM,), NB_DEV + 2 * HS, TILES_DEV + 1)
    fullest = jax.random.randint(key_full, (), 0, N_DOM)
    emptiest = (fullest + 1) % N_DOM
    counts = jnp.where(jnp.arange(N_DOM) == fullest, TILES_DEV, counts)
    counts = jnp.where(jnp.arange(N_DOM) == emptiest, NB_DEV + 2 * HS, counts).astype(jnp.int32)
    slot_index = jnp.arange(TILES_DEV, dtype=jnp.int32)[None, :]
    random_rows = jax.random.randint(key_rows, (N_DOM, TILES_DEV), 0, NB_DEV)
    random_cols = jax.random.randint(key_cols, (N_DOM, TILES_DEV), 0, NB_DEV + 2 * HS)
    diagonal = (slot_index >= 2 * HS) & (slot_index < 2 * HS + NB_DEV)
    row_table = jnp.where(diagonal, slot_index - 2 * HS, random_rows)
    col_table = jnp.where(slot_index < HS, slot_index, jnp.where(slot_index < 2 * HS, slot_index + NB_DEV, jnp.where(diagonal, slot_index - HS, random_cols)))
    orders = jax.vmap(lambda subkey: jax.random.permutation(subkey, TILES_DEV))(jax.random.split(key_order, N_DOM))
    scores = jnp.where(slot_index < counts[:, None], orders, TILES_DEV + slot_index)
    ranking = jnp.argsort(scores, axis=1)
    row_table = jnp.take_along_axis(row_table, ranking, axis=1).reshape(-1).astype(jnp.int32)
    col_table = jnp.take_along_axis(col_table, ranking, axis=1).reshape(-1).astype(jnp.int32)
    return (row_table, col_table, counts)


def draw_tile_rows(key, part):
    return graph_tables(key)[0]


def draw_tile_cols(key, part):
    return graph_tables(key)[1]


def draw_tile_count(key, part):
    return graph_tables(key)[2]


def halo_list(key, salt_value, shift_by):
    scores = jax.random.randint(jax.random.fold_in(key, salt_value), (N_DOM, NB_DEV), 0, 2 ** 20) * NB_DEV
    scores = scores + jnp.arange(NB_DEV, dtype=jnp.int32)[None, :]
    owner_index = (jnp.arange(N_DOM, dtype=jnp.int32) + shift_by) % N_DOM
    block_index = jnp.arange(NB_DEV, dtype=jnp.int32)[None, :]
    first_pick = (owner_index[:, None] == 0) & (block_index == 0)
    last_pick = (owner_index[:, None] == N_DOM - 1) & (block_index == NB_DEV - 1)
    scores = jnp.where(first_pick | last_pick, -1, scores)
    chosen = jnp.argsort(scores, axis=1)[:, :HS]
    return (owner_index[:, None] * NB_DEV + chosen).astype(jnp.int32)


def draw_halo_from_left(key, part):
    return halo_list(key, 23, N_DOM - 1)


def draw_halo_from_right(key, part):
    return halo_list(key, 29, 1)


def levels(key, shape, cuts, low, high):
    loudness, own = 1.0, jax.random.fold_in(key, 6)
    for dim, parts in cuts:
        heights = jnp.exp(jax.random.uniform(jax.random.fold_in(own, dim), (parts,), jnp.float32, low / len(cuts), high / len(cuts)))
        loudness = loudness * jnp.repeat(heights, shape[dim] // parts).reshape([-1 if axis == dim else 1 for axis in range(len(shape))])
    return loudness


def bell_draw(rng, extent, width, reach, pieces=(), kind=jnp.bfloat16):
    drawn = width * jax.random.normal(rng, extent, jnp.float32)
    if pieces:
        drawn = drawn * levels(rng, extent, pieces, -0.22, 0.18)
    return jnp.clip(drawn, -reach, reach).astype(kind)


def setup_inputs(seed: int = 0, part: int = 0) -> dict:
    splits = jax.random.split(jax.random.key(seed), 12)
    part_splits = jax.random.split(jax.random.fold_in(splits[11], part), 12)
    node_input = bell_draw(part_splits[0], (SAMP, NODES, LATENT_WIDTH), 1.0, 6.0, ((1, 4),))
    cotangent = bell_draw(part_splits[1], (SAMP, NODES, LATENT_WIDTH), 1.0, 6.0, ((1, 4),))
    w_one = bell_draw(splits[2], (LAYERS, 2 * LATENT_WIDTH, LATENT_WIDTH), (2 * LATENT_WIDTH) ** -0.5, 0.1875, ((0, 4),))
    w_two = bell_draw(splits[3], (LAYERS, LATENT_WIDTH, LATENT_WIDTH), LATENT_WIDTH ** -0.5, 0.25, ((0, 4),))
    gain = jnp.clip(1.0 + 0.18 * jax.random.normal(splits[4], (LAYERS, LATENT_WIDTH), jnp.float32), 0.1, 1.9)
    tile_weights = bell_draw(splits[5], (TILES, BLOCK, BLOCK), (4 * BLOCK) ** -0.5, 0.25, ((0, 4),))
    tile_rows = draw_tile_rows(jax.random.fold_in(splits[11], 71), part)
    tile_cols = draw_tile_cols(jax.random.fold_in(splits[11], 71), part)
    tile_count = draw_tile_count(jax.random.fold_in(splits[11], 71), part)
    halo_from_left = draw_halo_from_left(jax.random.fold_in(splits[11], 71), part)
    halo_from_right = draw_halo_from_right(jax.random.fold_in(splits[11], 71), part)
    return {"node_input": node_input, "cotangent": cotangent, "w_one": w_one, "w_two": w_two, "gain": gain, "tile_weights": tile_weights, "tile_rows": tile_rows, "tile_cols": tile_cols, "tile_count": tile_count, "halo_from_left": halo_from_left, "halo_from_right": halo_from_right}


EPSILON = 1e-05

def tile_tables(tile_rows, tile_cols, tile_count, halo_from_left, halo_from_right):
    device = (jnp.arange(TILES, dtype=jnp.int32) // TILES_DEV).astype(jnp.int32)
    global_rows = (device * NB_DEV + tile_rows).astype(jnp.int32)
    column = tile_cols
    left_ids = halo_from_left[device, jnp.clip(column, 0, HS - 1)]
    right_ids = halo_from_right[device, jnp.clip(column - HS - NB_DEV, 0, HS - 1)]
    global_cols = jnp.where(column < HS, left_ids, jnp.where(column < HS + NB_DEV, device * NB_DEV + column - HS, right_ids)).astype(jnp.int32)
    live_slots = (jnp.arange(TILES, dtype=jnp.int32) % TILES_DEV < tile_count[device]).astype(jnp.float32)
    return (global_rows, global_cols, live_slots)

def forward_layer(hidden_state, first_weight_matrix, second_weight_matrix, gain_row, tiles, global_rows, global_cols, live_slots):
    samples = hidden_state.shape[0]
    blocks = hidden_state.reshape(samples, NBLOCKS, BLOCK, LATENT_WIDTH)
    picked = jnp.take(blocks, global_cols, axis=1).astype(jnp.float32)
    product = jnp.einsum('tij,stjd->tsid', tiles.astype(jnp.float32), picked) * live_slots[:, None, None, None]
    summed = jax.ops.segment_sum(product, global_rows, num_segments=NBLOCKS)
    edge_sum_rows = jnp.transpose(summed, (1, 0, 2, 3)).reshape(samples, NODES, LATENT_WIDTH).astype(jnp.bfloat16)
    preactivation = jnp.einsum('uoc,ct->uot', hidden_state.astype(jnp.float32), first_weight_matrix[:LATENT_WIDTH].astype(jnp.float32))
    preactivation = preactivation + jnp.einsum('uoc,ct->uot', edge_sum_rows.astype(jnp.float32), first_weight_matrix[LATENT_WIDTH:].astype(jnp.float32))
    activation_rows = jax.nn.silu(preactivation).astype(jnp.bfloat16)
    mixed_output = jnp.einsum('uoc,ct->uot', activation_rows.astype(jnp.float32), second_weight_matrix.astype(jnp.float32))
    center = mixed_output - lax.optimization_barrier(jnp.mean(mixed_output, axis=-1, keepdims=True))
    inverse = lax.rsqrt(lax.optimization_barrier(jnp.mean(center * center, axis=-1, keepdims=True)) + EPSILON)
    normed = center * inverse
    result = (hidden_state.astype(jnp.float32) + normed * gain_row).astype(jnp.bfloat16)
    return (result, edge_sum_rows, preactivation, activation_rows, normed, inverse)

def backward_layer(upstream, hidden_state, edge_sum_rows, preactivation, activation_rows, normed, inverse, first_weight_matrix, second_weight_matrix, gain_row, tiles, global_rows, global_cols, live_slots):
    samples = hidden_state.shape[0]
    inbound_messages = upstream.astype(jnp.float32)
    gain_term = lax.optimization_barrier(jnp.sum(inbound_messages * normed, axis=(0, 1)))
    scaled = inbound_messages * gain_row
    output_gradient = (inverse * (scaled - lax.optimization_barrier(jnp.mean(scaled, axis=-1, keepdims=True)) - normed * lax.optimization_barrier(jnp.mean(scaled * normed, axis=-1, keepdims=True)))).astype(jnp.bfloat16)
    activation_gradient = jnp.einsum('bgp,vp->bgv', output_gradient.astype(jnp.float32), second_weight_matrix.astype(jnp.float32))
    sigmoid_pre = jax.nn.sigmoid(preactivation)
    preactivation_gradient = (activation_gradient * sigmoid_pre * (1.0 + preactivation * (1.0 - sigmoid_pre))).astype(jnp.bfloat16)
    gradient_node_rows = inbound_messages + jnp.einsum('bgp,vp->bgv', preactivation_gradient.astype(jnp.float32), first_weight_matrix[:LATENT_WIDTH].astype(jnp.float32))
    edge_sum_gradient = jnp.einsum('bgp,vp->bgv', preactivation_gradient.astype(jnp.float32), first_weight_matrix[LATENT_WIDTH:].astype(jnp.float32)).astype(jnp.bfloat16)
    grad_blocks = edge_sum_gradient.reshape(samples, NBLOCKS, BLOCK, LATENT_WIDTH)
    picked = jnp.take(grad_blocks, global_rows, axis=1).astype(jnp.float32)
    spread = jnp.einsum('tij,stid->tsjd', tiles.astype(jnp.float32), picked) * live_slots[:, None, None, None]
    summed = jax.ops.segment_sum(spread, global_cols, num_segments=NBLOCKS)
    gradient_node_rows = gradient_node_rows + jnp.transpose(summed, (1, 0, 2, 3)).reshape(samples, NODES, LATENT_WIDTH)
    stacked_layers = jnp.concatenate([hidden_state, edge_sum_rows], axis=2).astype(jnp.float32)
    first_weight_gradient = jnp.einsum('via,vid->ad', stacked_layers, preactivation_gradient.astype(jnp.float32))
    second_weight_gradient = jnp.einsum('via,vid->ad', activation_rows.astype(jnp.float32), output_gradient.astype(jnp.float32))
    return (gradient_node_rows.astype(jnp.bfloat16), first_weight_gradient, second_weight_gradient, gain_term)

def reference(node_input, cotangent, w_one, w_two, gain, tile_weights, tile_rows, tile_cols, tile_count, halo_from_left, halo_from_right):
    global_rows, global_cols, live_slots = tile_tables(tile_rows, tile_cols, tile_count, halo_from_left, halo_from_right)
    hidden_state = node_input
    inputs_kept = []
    residues = []
    outputs = []
    for layer in range(LAYERS):
        result, edge_sum_rows, preactivation, activation_rows, normed, inverse = forward_layer(hidden_state, w_one[layer], w_two[layer], gain[layer], tile_weights, global_rows, global_cols, live_slots)
        inputs_kept.append(hidden_state)
        residues.append((edge_sum_rows, preactivation, activation_rows, normed, inverse))
        outputs.append(result)
        hidden_state = result
    norm_factor = 1.0 / math.sqrt(SAMP * NODES)
    upstream = cotangent
    grads_in = [None] * LAYERS
    grads_one = [None] * LAYERS
    grads_two = [None] * LAYERS
    grads_gain = [None] * LAYERS
    for layer in range(LAYERS - 1, -1, -1):
        edge_sum_rows, preactivation, activation_rows, normed, inverse = residues[layer]
        gradient_node_rows, first_weight_gradient, second_weight_gradient, gain_term = backward_layer(upstream, inputs_kept[layer], edge_sum_rows, preactivation, activation_rows, normed, inverse, w_one[layer], w_two[layer], gain[layer], tile_weights, global_rows, global_cols, live_slots)
        grads_in[layer] = gradient_node_rows
        grads_one[layer] = first_weight_gradient * norm_factor
        grads_two[layer] = second_weight_gradient * norm_factor
        grads_gain[layer] = gain_term * norm_factor
        upstream = gradient_node_rows
    return (jnp.stack(outputs), jnp.stack(grads_in), jnp.stack(grads_one), jnp.stack(grads_two), jnp.stack(grads_gain))
```

```python
import math

import jax
import jax.numpy as jnp
from jax import lax
from jax.sharding import PartitionSpec as P

EPSILON = 1e-05
HIGHEST_PRECISION = lax.Precision.HIGHEST
F32 = jnp.float32
BF16 = jnp.bfloat16


def pick_blocks(blocks, index, count):
    parts = [lax.dynamic_index_in_dim(blocks, index[i], axis=1, keepdims=False) for i in range(count)]
    return jnp.concatenate(parts, axis=1)


def add_blocks(blocks, index, count, values):
    samples, nb, blk, width = blocks.shape
    values = values.reshape(samples, count, blk, width).astype(F32)
    for i in range(count):
        hit = (jnp.arange(nb) == index[i])[None, :, None, None]
        blocks = blocks + jnp.where(hit, values[:, i][:, None], 0.0)
    return blocks


def shards(
    node_input,
    cotangent,
    w_one,
    w_two,
    gain,
    tile_weights,
    tile_rows,
    tile_cols,
    tile_count,
    halo_from_left,
    halo_from_right,
):
    sections = lax.axis_size("section")
    section_index = lax.axis_index("section")
    domains = lax.axis_size("dom")
    domain_index = lax.axis_index("dom")
    samples, node_rows, width = node_input.shape
    slot_count, blk, _ = tile_weights.shape
    nb = node_rows // blk
    hs = halo_from_left.shape[1]
    ext = nb + 2 * hs
    margin = hs * blk
    offset = domain_index * nb
    send_right = jnp.take(halo_from_left, (domain_index + 1) % domains, axis=0) - offset
    send_left = jnp.take(halo_from_right, (domain_index + domains - 1) % domains, axis=0) - offset

    live = (jnp.arange(slot_count) < tile_count[0]).astype(F32)
    row_oh = (tile_rows[:, None] == jnp.arange(nb)[None, :]).astype(F32) * live[:, None]
    col_oh = (tile_cols[:, None] == jnp.arange(ext)[None, :]).astype(F32)
    pair = (row_oh[:, :, None] * col_oh[:, None, :]).reshape(slot_count, nb * ext)
    adj = jnp.einsum("tp,tij->pij", pair, tile_weights.astype(F32), precision=HIGHEST_PRECISION)
    adj = adj.reshape(nb, ext, blk, blk).transpose(0, 2, 1, 3).reshape(nb * blk, ext * blk)
    adj_hi = adj.astype(BF16)
    adj_lo = (adj - adj_hi.astype(F32)).astype(BF16)
    adj2 = jnp.concatenate([adj_hi, adj_lo], axis=0)

    w_a = w_one[0, :width]
    w_b = w_one[0, width:]
    w_2 = w_two[0]
    gain_row = gain[0]

    dom_up = [(i, (i + 1) % domains) for i in range(domains)]
    dom_down = [((i + 1) % domains, i) for i in range(domains)]
    sec_up = [(i, i + 1) for i in range(sections - 1)]
    sec_down = [(i + 1, i) for i in range(sections - 1)]

    def linear(d, s):
        return d * sections + s

    diag_right = [
        (linear(d, s), linear((d + 1) % domains, s + 1))
        for d in range(domains)
        for s in range(sections - 1)
    ]
    diag_left = [
        (linear(d, s), linear((d + domains - 1) % domains, s + 1))
        for d in range(domains)
        for s in range(sections - 1)
    ]
    both = ("dom", "section")

    def forward_layer(h, left, right):
        h_ext = jnp.concatenate([left, h, right], axis=1)
        agg2 = jnp.einsum("ij,sjd->sid", adj2, h_ext, preferred_element_type=F32)
        agg = (agg2[:, : nb * blk] + agg2[:, nb * blk :]).astype(BF16)
        pre = jnp.einsum("sic,ct->sit", h, w_a, preferred_element_type=F32)
        pre = pre + jnp.einsum("sic,ct->sit", agg, w_b, preferred_element_type=F32)
        act = jax.nn.silu(pre).astype(BF16)
        mixed = jnp.einsum("sic,ct->sit", act, w_2, preferred_element_type=F32)
        center = mixed - jnp.mean(mixed, axis=-1, keepdims=True)
        rstd = lax.rsqrt(jnp.mean(center * center, axis=-1, keepdims=True) + EPSILON)
        normed = center * rstd
        out = (h.astype(F32) + normed * gain_row).astype(BF16)
        return out, (h, agg, pre, act, normed, rstd)

    in_blocks = node_input.reshape(samples, nb, blk, width)
    left = lax.ppermute(pick_blocks(in_blocks, send_right, hs), "dom", dom_up)
    right = lax.ppermute(pick_blocks(in_blocks, send_left, hs), "dom", dom_down)
    h = node_input
    saved = None
    saved_out = None
    for tick in range(sections):
        out, res = forward_layer(h, left, right)
        if saved is None:
            saved = res
            saved_out = out
        else:
            mine = section_index == tick
            saved = tuple(jnp.where(mine, a, b) for a, b in zip(res, saved))
            saved_out = jnp.where(mine, out, saved_out)
        if tick + 1 < sections:
            out_blocks = out.reshape(samples, nb, blk, width)
            h = lax.ppermute(out, "section", sec_up)
            left = lax.ppermute(pick_blocks(out_blocks, send_right, hs), both, diag_right)
            right = lax.ppermute(pick_blocks(out_blocks, send_left, hs), both, diag_left)

    h_in, agg, pre, act, normed, rstd = saved

    g = cotangent
    grad_in = None
    dpre_keep = None
    dout_keep = None
    gain_keep = None
    for tick in range(sections):
        gf = g.astype(F32)
        gain_term = jnp.sum(gf * normed, axis=(0, 1))
        dn = gf * gain_row
        dout = (
            rstd
            * (
                dn
                - jnp.mean(dn, axis=-1, keepdims=True)
                - normed * jnp.mean(dn * normed, axis=-1, keepdims=True)
            )
        ).astype(BF16)
        dact = jnp.einsum("sip,vp->siv", dout, w_2, preferred_element_type=F32)
        sig = jax.nn.sigmoid(pre)
        dpre = (dact * sig * (1.0 + pre * (1.0 - sig))).astype(BF16)
        gnode = gf + jnp.einsum("sip,vp->siv", dpre, w_a, preferred_element_type=F32)
        dagg = jnp.einsum("sip,vp->siv", dpre, w_b, preferred_element_type=F32).astype(BF16)
        spread = jnp.einsum(
            "ij,sid->sjd", adj2, jnp.concatenate([dagg, dagg], axis=1), preferred_element_type=F32
        )
        left_grad = spread[:, :margin].astype(BF16)
        right_grad = spread[:, margin + nb * blk :].astype(BF16)
        own = gnode + spread[:, margin : margin + nb * blk]
        from_right = lax.ppermute(left_grad, "dom", dom_down)
        from_left = lax.ppermute(right_grad, "dom", dom_up)
        own_blocks = own.reshape(samples, nb, blk, width)
        own_blocks = add_blocks(own_blocks, send_right, hs, from_right)
        own_blocks = add_blocks(own_blocks, send_left, hs, from_left)
        g_new = own_blocks.reshape(samples, node_rows, width).astype(BF16)
        if grad_in is None:
            grad_in, dpre_keep, dout_keep = g_new, dpre, dout
            gain_keep = gain_term
        else:
            mine = section_index == sections - 1 - tick
            grad_in = jnp.where(mine, g_new, grad_in)
            dpre_keep = jnp.where(mine, dpre, dpre_keep)
            dout_keep = jnp.where(mine, dout, dout_keep)
            gain_keep = jnp.where(mine, gain_term, gain_keep)
        if tick + 1 < sections:
            g = lax.ppermute(g_new, "section", sec_down)

    norm_factor = 1.0 / math.sqrt(samples * node_rows * domains)
    stacked = jnp.concatenate([h_in, agg], axis=2)
    gw1 = jnp.einsum("via,vid->ad", stacked, dpre_keep, preferred_element_type=F32)
    gw2 = jnp.einsum("via,vid->ad", act, dout_keep, preferred_element_type=F32)
    r1 = gw1.shape[0] // domains
    r2 = gw2.shape[0] // domains
    r3 = gain_keep.shape[0] // domains
    packed = jnp.concatenate(
        [
            gw1.reshape(domains, r1 * width),
            gw2.reshape(domains, r2 * width),
            gain_keep.reshape(domains, r3),
        ],
        axis=1,
    ).astype(BF16)
    reduced = lax.psum_scatter(packed, "dom", scatter_dimension=0, tiled=True)
    reduced = reduced[0].astype(F32) * norm_factor
    g1 = reduced[: r1 * width].reshape(r1, width)
    g2 = reduced[r1 * width : r1 * width + r2 * width].reshape(r2, width)
    g3 = reduced[r1 * width + r2 * width :]
    return (
        saved_out[None],
        grad_in[None],
        g1[None],
        g2[None],
        g3[None],
    )


def solution(mesh):
    return jax.shard_map(
        shards,
        mesh=mesh,
        in_specs=(
            P("groups", "dom", None),
            P("groups", "dom", None),
            P("section", None, None),
            P("section", None, None),
            P("section", None),
            P("dom", None, None),
            P("dom"),
            P("dom"),
            P("dom"),
            P(),
            P(),
        ),
        out_specs=(
            P("section", "groups", "dom", None),
            P("section", "groups", "dom", None),
            P("section", "dom", "groups"),
            P("section", "dom", "groups"),
            P("section", ("groups", "dom")),
        ),
        check_vma=False,
    )
```

```python
import math

import jax
import jax.numpy as jnp
from jax import lax
from jax.sharding import PartitionSpec as P

EPSILON = 1e-05
HIGHEST_PRECISION = lax.Precision.HIGHEST
F32 = jnp.float32
BF16 = jnp.bfloat16


def pick_blocks(blocks, index, count):
    parts = [lax.dynamic_index_in_dim(blocks, index[i], axis=1, keepdims=False) for i in range(count)]
    return jnp.concatenate(parts, axis=1)


def add_blocks(blocks, index, count, values):
    samples, nb, blk, width = blocks.shape
    values = values.reshape(samples, count, blk, width).astype(F32)
    for i in range(count):
        hit = (jnp.arange(nb) == index[i])[None, :, None, None]
        blocks = blocks + jnp.where(hit, values[:, i][:, None], 0.0)
    return blocks


def shards(
    node_input,
    cotangent,
    w_one,
    w_two,
    gain,
    tile_weights,
    tile_rows,
    tile_cols,
    tile_count,
    halo_from_left,
    halo_from_right,
):
    sections = lax.axis_size("section")
    section_index = lax.axis_index("section")
    domains = lax.axis_size("dom")
    domain_index = lax.axis_index("dom")
    samples, node_rows, width = node_input.shape
    slot_count, blk, _ = tile_weights.shape
    nb = node_rows // blk
    hs = halo_from_left.shape[1]
    ext = nb + 2 * hs
    margin = hs * blk
    offset = domain_index * nb
    send_right = jnp.take(halo_from_left, (domain_index + 1) % domains, axis=0) - offset
    send_left = jnp.take(halo_from_right, (domain_index + domains - 1) % domains, axis=0) - offset

    live = (jnp.arange(slot_count) < tile_count[0]).astype(F32)
    row_oh = (tile_rows[:, None] == jnp.arange(nb)[None, :]).astype(F32) * live[:, None]
    col_oh = (tile_cols[:, None] == jnp.arange(ext)[None, :]).astype(F32)
    pair = (row_oh[:, :, None] * col_oh[:, None, :]).reshape(slot_count, nb * ext)
    adj = jnp.einsum("tp,tij->pij", pair, tile_weights.astype(F32), precision=HIGHEST_PRECISION)
    adj = adj.reshape(nb, ext, blk, blk).transpose(0, 2, 1, 3).reshape(nb * blk, ext * blk)
    adj_hi = adj.astype(BF16)
    adj_lo = (adj - adj_hi.astype(F32)).astype(BF16)
    adj2 = jnp.concatenate([adj_hi, adj_lo], axis=0)

    w_a = w_one[0, :width]
    w_b = w_one[0, width:]
    w_2 = w_two[0]
    gain_row = gain[0]

    dom_up = [(i, (i + 1) % domains) for i in range(domains)]
    dom_down = [((i + 1) % domains, i) for i in range(domains)]
    sec_up = [(i, i + 1) for i in range(sections - 1)]
    sec_down = [(i + 1, i) for i in range(sections - 1)]

    def linear(d, s):
        return d * sections + s

    diag_right = [
        (linear(d, s), linear((d + 1) % domains, s + 1))
        for d in range(domains)
        for s in range(sections - 1)
    ]
    diag_left = [
        (linear(d, s), linear((d + domains - 1) % domains, s + 1))
        for d in range(domains)
        for s in range(sections - 1)
    ]
    diag_down_left = [
        (linear(d, s + 1), linear((d + domains - 1) % domains, s))
        for d in range(domains)
        for s in range(sections - 1)
    ]
    diag_down_right = [
        (linear(d, s + 1), linear((d + 1) % domains, s))
        for d in range(domains)
        for s in range(sections - 1)
    ]
    both = ("dom", "section")

    def forward_layer(h, left, right):
        h_ext = jnp.concatenate([left, h, right], axis=1)
        agg2 = jnp.einsum("ij,sjd->sid", adj2, h_ext, preferred_element_type=F32)
        agg = (agg2[:, : nb * blk] + agg2[:, nb * blk :]).astype(BF16)
        pre = jnp.einsum("sic,ct->sit", h, w_a, preferred_element_type=F32)
        pre = pre + jnp.einsum("sic,ct->sit", agg, w_b, preferred_element_type=F32)
        act = jax.nn.silu(pre).astype(BF16)
        mixed = jnp.einsum("sic,ct->sit", act, w_2, preferred_element_type=F32)
        center = mixed - jnp.mean(mixed, axis=-1, keepdims=True)
        rstd = lax.rsqrt(jnp.mean(center * center, axis=-1, keepdims=True) + EPSILON)
        normed = center * rstd
        out = (h.astype(F32) + normed * gain_row).astype(BF16)
        return out, (h, agg, pre, act, normed, rstd)

    in_blocks = node_input.reshape(samples, nb, blk, width)
    left = lax.ppermute(pick_blocks(in_blocks, send_right, hs), "dom", dom_up)
    right = lax.ppermute(pick_blocks(in_blocks, send_left, hs), "dom", dom_down)
    h = node_input
    saved = None
    saved_out = None
    for tick in range(sections):
        out, res = forward_layer(h, left, right)
        if saved is None:
            saved = res
            saved_out = out
        else:
            mine = section_index == tick
            saved = tuple(jnp.where(mine, a, b) for a, b in zip(res, saved))
            saved_out = jnp.where(mine, out, saved_out)
        if tick + 1 < sections:
            out_blocks = out.reshape(samples, nb, blk, width)
            h = lax.ppermute(out, "section", sec_up)
            left = lax.ppermute(pick_blocks(out_blocks, send_right, hs), both, diag_right)
            right = lax.ppermute(pick_blocks(out_blocks, send_left, hs), both, diag_left)

    h_in, agg, pre, act, normed, rstd = saved

    g = cotangent
    grad_in = None
    dpre_keep = None
    dout_keep = None
    gain_keep = None
    for tick in range(sections):
        gf = g.astype(F32)
        gain_term = jnp.sum(gf * normed, axis=(0, 1))
        dn = gf * gain_row
        dout = (
            rstd
            * (
                dn
                - jnp.mean(dn, axis=-1, keepdims=True)
                - normed * jnp.mean(dn * normed, axis=-1, keepdims=True)
            )
        ).astype(BF16)
        dact = jnp.einsum("sip,vp->siv", dout, w_2, preferred_element_type=F32)
        sig = jax.nn.sigmoid(pre)
        dpre = (dact * sig * (1.0 + pre * (1.0 - sig))).astype(BF16)
        gnode = gf + jnp.einsum("sip,vp->siv", dpre, w_a, preferred_element_type=F32)
        dagg = jnp.einsum("sip,vp->siv", dpre, w_b, preferred_element_type=F32).astype(BF16)
        spread = jnp.einsum(
            "ij,sid->sjd", adj2, jnp.concatenate([dagg, dagg], axis=1), preferred_element_type=F32
        )
        left_grad = spread[:, :margin].astype(BF16)
        right_grad = spread[:, margin + nb * blk :].astype(BF16)
        own = gnode + spread[:, margin : margin + nb * blk]

        def finish(partial, from_right, from_left):
            blocks = partial.reshape(samples, nb, blk, width)
            blocks = add_blocks(blocks, send_right, hs, from_right)
            blocks = add_blocks(blocks, send_left, hs, from_left)
            return blocks.reshape(samples, node_rows, width).astype(BF16)

        g_new = finish(
            own,
            lax.ppermute(left_grad, "dom", dom_down),
            lax.ppermute(right_grad, "dom", dom_up),
        )
        if grad_in is None:
            grad_in, dpre_keep, dout_keep = g_new, dpre, dout
            gain_keep = gain_term
        else:
            mine = section_index == sections - 1 - tick
            grad_in = jnp.where(mine, g_new, grad_in)
            dpre_keep = jnp.where(mine, dpre, dpre_keep)
            dout_keep = jnp.where(mine, dout, dout_keep)
            gain_keep = jnp.where(mine, gain_term, gain_keep)
        if tick + 1 < sections:
            g = finish(
                lax.ppermute(own, "section", sec_down),
                lax.ppermute(left_grad, both, diag_down_left),
                lax.ppermute(right_grad, both, diag_down_right),
            )

    norm_factor = 1.0 / math.sqrt(samples * node_rows * domains)
    stacked = jnp.concatenate([h_in, agg], axis=2)
    gw1 = jnp.einsum("via,vid->ad", stacked, dpre_keep, preferred_element_type=F32)
    gw2 = jnp.einsum("via,vid->ad", act, dout_keep, preferred_element_type=F32)
    r1 = gw1.shape[0] // domains
    r2 = gw2.shape[0] // domains
    r3 = gain_keep.shape[0] // domains
    pad_rows = 16
    gain_rows = jnp.pad(gain_keep.reshape(domains, 1, r3), ((0, 0), (0, pad_rows - 1), (0, width - r3)))
    packed = jnp.concatenate(
        [
            gw1.reshape(domains, r1, width),
            gw2.reshape(domains, r2, width),
            gain_rows,
        ],
        axis=1,
    ).astype(BF16)
    packed = packed.reshape(domains * (r1 + r2 + pad_rows), width)
    reduced = lax.psum_scatter(packed, "dom", scatter_dimension=0, tiled=True)
    reduced = reduced.astype(F32) * norm_factor
    g1 = reduced[:r1]
    g2 = reduced[r1 : r1 + r2]
    g3 = reduced[r1 + r2, :r3]
    return (
        saved_out[None],
        grad_in[None],
        g1[None],
        g2[None],
        g3[None],
    )


def solution(mesh):
    return jax.shard_map(
        shards,
        mesh=mesh,
        in_specs=(
            P("groups", "dom", None),
            P("groups", "dom", None),
            P("section", None, None),
            P("section", None, None),
            P("section", None),
            P("dom", None, None),
            P("dom"),
            P("dom"),
            P("dom"),
            P(),
            P(),
        ),
        out_specs=(
            P("section", "groups", "dom", None),
            P("section", "groups", "dom", None),
            P("section", "dom", "groups"),
            P("section", "dom", "groups"),
            P("section", ("groups", "dom")),
        ),
        check_vma=False,
    )
```

```python
import math

import jax
import jax.numpy as jnp
from jax import lax
from jax.sharding import PartitionSpec as P

EPSILON = 1e-05
HIGHEST_PRECISION = lax.Precision.HIGHEST
F32 = jnp.float32
BF16 = jnp.bfloat16


def pick_blocks(blocks, index, count):
    parts = [lax.dynamic_index_in_dim(blocks, index[i], axis=1, keepdims=False) for i in range(count)]
    return jnp.concatenate(parts, axis=1)


def add_blocks(blocks, index, count, values):
    samples, nb, blk, width = blocks.shape
    values = values.reshape(samples, count, blk, width).astype(F32)
    for i in range(count):
        hit = (jnp.arange(nb) == index[i])[None, :, None, None]
        blocks = blocks + jnp.where(hit, values[:, i][:, None], 0.0)
    return blocks


def halving_reduce_scatter(x, axis, devices, index):
    if devices & (devices - 1):
        return lax.psum_scatter(x, axis, scatter_dimension=0, tiled=True)
    rows = x.shape[0] // devices
    cur = x.reshape(devices, rows, x.shape[1]).astype(F32)
    dist = 1
    while dist < devices:
        cur = cur.reshape(cur.shape[0] // 2, 2, rows, x.shape[1])
        bit = (index // dist) % 2
        low, high = cur[:, 0], cur[:, 1]
        keep = jnp.where(bit == 0, low, high)
        send = jnp.where(bit == 0, high, low).astype(x.dtype)
        pairs = [(i, i ^ dist) for i in range(devices)]
        recv = lax.ppermute(send, axis, pairs)
        cur = keep + recv.astype(F32)
        dist *= 2
    return cur[0]


def shards(
    node_input,
    cotangent,
    w_one,
    w_two,
    gain,
    tile_weights,
    tile_rows,
    tile_cols,
    tile_count,
    halo_from_left,
    halo_from_right,
):
    sections = lax.axis_size("section")
    section_index = lax.axis_index("section")
    domains = lax.axis_size("dom")
    domain_index = lax.axis_index("dom")
    samples, node_rows, width = node_input.shape
    slot_count, blk, _ = tile_weights.shape
    nb = node_rows // blk
    hs = halo_from_left.shape[1]
    ext = nb + 2 * hs
    margin = hs * blk
    offset = domain_index * nb
    send_right = jnp.take(halo_from_left, (domain_index + 1) % domains, axis=0) - offset
    send_left = jnp.take(halo_from_right, (domain_index + domains - 1) % domains, axis=0) - offset

    live = (jnp.arange(slot_count) < tile_count[0]).astype(F32)
    row_oh = (tile_rows[:, None] == jnp.arange(nb)[None, :]).astype(F32) * live[:, None]
    col_oh = (tile_cols[:, None] == jnp.arange(ext)[None, :]).astype(F32)
    pair = (row_oh[:, :, None] * col_oh[:, None, :]).reshape(slot_count, nb * ext)
    adj = jnp.einsum("tp,tij->pij", pair, tile_weights.astype(F32), precision=HIGHEST_PRECISION)
    adj = adj.reshape(nb, ext, blk, blk).transpose(0, 2, 1, 3).reshape(nb * blk, ext * blk)
    adj_hi = adj.astype(BF16)
    adj_lo = (adj - adj_hi.astype(F32)).astype(BF16)
    adj2 = jnp.concatenate([adj_hi, adj_lo], axis=0)

    w_a = w_one[0, :width]
    w_b = w_one[0, width:]
    w_2 = w_two[0]
    gain_row = gain[0]

    dom_up = [(i, (i + 1) % domains) for i in range(domains)]
    dom_down = [((i + 1) % domains, i) for i in range(domains)]
    sec_up = [(i, i + 1) for i in range(sections - 1)]
    sec_down = [(i + 1, i) for i in range(sections - 1)]

    def linear(d, s):
        return d * sections + s

    diag_right = [
        (linear(d, s), linear((d + 1) % domains, s + 1))
        for d in range(domains)
        for s in range(sections - 1)
    ]
    diag_left = [
        (linear(d, s), linear((d + domains - 1) % domains, s + 1))
        for d in range(domains)
        for s in range(sections - 1)
    ]
    diag_down_left = [
        (linear(d, s + 1), linear((d + domains - 1) % domains, s))
        for d in range(domains)
        for s in range(sections - 1)
    ]
    diag_down_right = [
        (linear(d, s + 1), linear((d + 1) % domains, s))
        for d in range(domains)
        for s in range(sections - 1)
    ]
    both = ("dom", "section")

    def forward_layer(h, left, right):
        h_ext = jnp.concatenate([left, h, right], axis=1)
        agg2 = jnp.einsum("ij,sjd->sid", adj2, h_ext, preferred_element_type=F32)
        agg = (agg2[:, : nb * blk] + agg2[:, nb * blk :]).astype(BF16)
        pre = jnp.einsum("sic,ct->sit", h, w_a, preferred_element_type=F32)
        pre = pre + jnp.einsum("sic,ct->sit", agg, w_b, preferred_element_type=F32)
        act = jax.nn.silu(pre).astype(BF16)
        mixed = jnp.einsum("sic,ct->sit", act, w_2, preferred_element_type=F32)
        center = mixed - jnp.mean(mixed, axis=-1, keepdims=True)
        rstd = lax.rsqrt(jnp.mean(center * center, axis=-1, keepdims=True) + EPSILON)
        normed = center * rstd
        out = (h.astype(F32) + normed * gain_row).astype(BF16)
        return out, (h, agg, pre, act, normed, rstd)

    in_blocks = node_input.reshape(samples, nb, blk, width)
    left = lax.ppermute(pick_blocks(in_blocks, send_right, hs), "dom", dom_up)
    right = lax.ppermute(pick_blocks(in_blocks, send_left, hs), "dom", dom_down)
    h = node_input
    saved = None
    saved_out = None
    for tick in range(sections):
        out, res = forward_layer(h, left, right)
        if saved is None:
            saved = res
            saved_out = out
        else:
            mine = section_index == tick
            saved = tuple(jnp.where(mine, a, b) for a, b in zip(res, saved))
            saved_out = jnp.where(mine, out, saved_out)
        if tick + 1 < sections:
            out_blocks = out.reshape(samples, nb, blk, width)
            h = lax.ppermute(out, "section", sec_up)
            left = lax.ppermute(pick_blocks(out_blocks, send_right, hs), both, diag_right)
            right = lax.ppermute(pick_blocks(out_blocks, send_left, hs), both, diag_left)

    h_in, agg, pre, act, normed, rstd = saved

    g = cotangent
    grad_in = None
    dpre_keep = None
    dout_keep = None
    gain_keep = None
    for tick in range(sections):
        gf = g.astype(F32)
        gain_term = jnp.sum(gf * normed, axis=(0, 1))
        dn = gf * gain_row
        dout = (
            rstd
            * (
                dn
                - jnp.mean(dn, axis=-1, keepdims=True)
                - normed * jnp.mean(dn * normed, axis=-1, keepdims=True)
            )
        ).astype(BF16)
        dact = jnp.einsum("sip,vp->siv", dout, w_2, preferred_element_type=F32)
        sig = jax.nn.sigmoid(pre)
        dpre = (dact * sig * (1.0 + pre * (1.0 - sig))).astype(BF16)
        gnode = gf + jnp.einsum("sip,vp->siv", dpre, w_a, preferred_element_type=F32)
        dagg = jnp.einsum("sip,vp->siv", dpre, w_b, preferred_element_type=F32).astype(BF16)
        spread = jnp.einsum(
            "ij,sid->sjd", adj2, jnp.concatenate([dagg, dagg], axis=1), preferred_element_type=F32
        )
        left_grad = spread[:, :margin].astype(BF16)
        right_grad = spread[:, margin + nb * blk :].astype(BF16)
        own = gnode + spread[:, margin : margin + nb * blk]

        def finish(partial, from_right, from_left):
            blocks = partial.reshape(samples, nb, blk, width)
            blocks = add_blocks(blocks, send_right, hs, from_right)
            blocks = add_blocks(blocks, send_left, hs, from_left)
            return blocks.reshape(samples, node_rows, width).astype(BF16)

        g_new = finish(
            own,
            lax.ppermute(left_grad, "dom", dom_down),
            lax.ppermute(right_grad, "dom", dom_up),
        )
        if grad_in is None:
            grad_in, dpre_keep, dout_keep = g_new, dpre, dout
            gain_keep = gain_term
        else:
            mine = section_index == sections - 1 - tick
            grad_in = jnp.where(mine, g_new, grad_in)
            dpre_keep = jnp.where(mine, dpre, dpre_keep)
            dout_keep = jnp.where(mine, dout, dout_keep)
            gain_keep = jnp.where(mine, gain_term, gain_keep)
        if tick + 1 < sections:
            g = finish(
                lax.ppermute(own, "section", sec_down),
                lax.ppermute(left_grad, both, diag_down_left),
                lax.ppermute(right_grad, both, diag_down_right),
            )

    norm_factor = 1.0 / math.sqrt(samples * node_rows * domains)
    stacked = jnp.concatenate([h_in, agg], axis=2)
    gw1 = jnp.einsum("via,vid->ad", stacked, dpre_keep, preferred_element_type=F32)
    gw2 = jnp.einsum("via,vid->ad", act, dout_keep, preferred_element_type=F32)
    r1 = gw1.shape[0] // domains
    r2 = gw2.shape[0] // domains
    r3 = gain_keep.shape[0] // domains
    pad_rows = 16
    gain_rows = jnp.pad(gain_keep.reshape(domains, 1, r3), ((0, 0), (0, pad_rows - 1), (0, width - r3)))
    packed = jnp.concatenate(
        [
            gw1.reshape(domains, r1, width),
            gw2.reshape(domains, r2, width),
            gain_rows,
        ],
        axis=1,
    ).astype(BF16)
    packed = packed.reshape(domains * (r1 + r2 + pad_rows), width)
    reduced = halving_reduce_scatter(packed, "dom", domains, domain_index)
    reduced = reduced.astype(F32) * norm_factor
    g1 = reduced[:r1]
    g2 = reduced[r1 : r1 + r2]
    g3 = reduced[r1 + r2, :r3]
    return (
        saved_out[None],
        grad_in[None],
        g1[None],
        g2[None],
        g3[None],
    )


def solution(mesh):
    return jax.shard_map(
        shards,
        mesh=mesh,
        in_specs=(
            P("groups", "dom", None),
            P("groups", "dom", None),
            P("section", None, None),
            P("section", None, None),
            P("section", None),
            P("dom", None, None),
            P("dom"),
            P("dom"),
            P("dom"),
            P(),
            P(),
        ),
        out_specs=(
            P("section", "groups", "dom", None),
            P("section", "groups", "dom", None),
            P("section", "dom", "groups"),
            P("section", "dom", "groups"),
            P("section", ("groups", "dom")),
        ),
        check_vma=False,
    )
```

```python
import math

import jax
import jax.numpy as jnp
from jax import lax
from jax.sharding import PartitionSpec as P

EPSILON = 1e-05
HIGHEST_PRECISION = lax.Precision.HIGHEST
F32 = jnp.float32
BF16 = jnp.bfloat16


def pick_blocks(blocks, index, count):
    parts = [lax.dynamic_index_in_dim(blocks, index[i], axis=1, keepdims=False) for i in range(count)]
    return jnp.concatenate(parts, axis=1)


def add_blocks(blocks, index, count, values):
    samples, nb, blk, width = blocks.shape
    values = values.reshape(samples, count, blk, width).astype(F32)
    for i in range(count):
        hit = (jnp.arange(nb) == index[i])[None, :, None, None]
        blocks = blocks + jnp.where(hit, values[:, i][:, None], 0.0)
    return blocks


def halving_reduce_scatter(x, axis, devices, index):
    if devices & (devices - 1):
        return lax.psum_scatter(x, axis, scatter_dimension=0, tiled=True)
    rows = x.shape[0] // devices
    cur = x.reshape(devices, rows, x.shape[1]).astype(F32)
    dist = 1
    while dist < devices:
        cur = cur.reshape(cur.shape[0] // 2, 2, rows, x.shape[1])
        bit = (index // dist) % 2
        low, high = cur[:, 0], cur[:, 1]
        keep = jnp.where(bit == 0, low, high)
        send = jnp.where(bit == 0, high, low).astype(x.dtype)
        pairs = [(i, i ^ dist) for i in range(devices)]
        recv = lax.ppermute(send, axis, pairs)
        cur = keep + recv.astype(F32)
        dist *= 2
    return cur[0]


def shards(
    node_input,
    cotangent,
    w_one,
    w_two,
    gain,
    tile_weights,
    tile_rows,
    tile_cols,
    tile_count,
    halo_from_left,
    halo_from_right,
):
    sections = lax.axis_size("section")
    section_index = lax.axis_index("section")
    domains = lax.axis_size("dom")
    domain_index = lax.axis_index("dom")
    samples, node_rows, width = node_input.shape
    slot_count, blk, _ = tile_weights.shape
    nb = node_rows // blk
    hs = halo_from_left.shape[1]
    ext = nb + 2 * hs
    margin = hs * blk
    offset = domain_index * nb
    send_right = jnp.take(halo_from_left, (domain_index + 1) % domains, axis=0) - offset
    send_left = jnp.take(halo_from_right, (domain_index + domains - 1) % domains, axis=0) - offset

    live = (jnp.arange(slot_count) < tile_count[0]).astype(F32)
    row_oh = (tile_rows[:, None] == jnp.arange(nb)[None, :]).astype(F32) * live[:, None]
    col_oh = (tile_cols[:, None] == jnp.arange(ext)[None, :]).astype(F32)
    pair = (row_oh[:, :, None] * col_oh[:, None, :]).reshape(slot_count, nb * ext)
    adj = jnp.einsum("tp,tij->pij", pair, tile_weights.astype(F32), precision=HIGHEST_PRECISION)
    adj = adj.reshape(nb, ext, blk, blk).transpose(0, 2, 1, 3).reshape(nb * blk, ext * blk)
    adj_hi = adj.astype(BF16)
    adj_lo = (adj - adj_hi.astype(F32)).astype(BF16)
    adj2 = jnp.concatenate([adj_hi, adj_lo], axis=0)

    w_a = w_one[0, :width]
    w_b = w_one[0, width:]
    w_2 = w_two[0]
    gain_row = gain[0]

    both = ("dom", "section")

    def linear(d, s):
        return d * sections + s

    def route(src_section, dst_section, shift):
        return [
            (linear(d, src_section), linear((d + shift) % domains, dst_section))
            for d in range(domains)
        ]

    def forward_layer(h, left, right):
        h_ext = jnp.concatenate([left, h, right], axis=1)
        agg2 = jnp.einsum("ij,sjd->sid", adj2, h_ext, preferred_element_type=F32)
        agg = (agg2[:, : nb * blk] + agg2[:, nb * blk :]).astype(BF16)
        pre = jnp.einsum("sic,ct->sit", h, w_a, preferred_element_type=F32)
        pre = pre + jnp.einsum("sic,ct->sit", agg, w_b, preferred_element_type=F32)
        act = jax.nn.silu(pre).astype(BF16)
        mixed = jnp.einsum("sic,ct->sit", act, w_2, preferred_element_type=F32)
        center = mixed - jnp.mean(mixed, axis=-1, keepdims=True)
        rstd = lax.rsqrt(jnp.mean(center * center, axis=-1, keepdims=True) + EPSILON)
        normed = center * rstd
        out = (h.astype(F32) + normed * gain_row).astype(BF16)
        return out, (h, agg, pre, act, normed, rstd)

    in_blocks = node_input.reshape(samples, nb, blk, width)
    left = lax.ppermute(pick_blocks(in_blocks, send_right, hs), both, route(0, 0, 1))
    right = lax.ppermute(pick_blocks(in_blocks, send_left, hs), both, route(0, 0, -1))
    h = node_input
    saved = None
    saved_out = None
    for tick in range(sections):
        out, res = forward_layer(h, left, right)
        if saved is None:
            saved = res
            saved_out = out
        else:
            mine = section_index == tick
            saved = tuple(jnp.where(mine, a, b) for a, b in zip(res, saved))
            saved_out = jnp.where(mine, out, saved_out)
        if tick + 1 < sections:
            out_blocks = out.reshape(samples, nb, blk, width)
            h = lax.ppermute(out, both, route(tick, tick + 1, 0))
            left = lax.ppermute(pick_blocks(out_blocks, send_right, hs), both, route(tick, tick + 1, 1))
            right = lax.ppermute(pick_blocks(out_blocks, send_left, hs), both, route(tick, tick + 1, -1))

    h_in, agg, pre, act, normed, rstd = saved

    g = cotangent
    grad_in = None
    dpre_keep = None
    dout_keep = None
    gain_keep = None
    for tick in range(sections):
        gf = g.astype(F32)
        gain_term = jnp.sum(gf * normed, axis=(0, 1))
        dn = gf * gain_row
        dout = (
            rstd
            * (
                dn
                - jnp.mean(dn, axis=-1, keepdims=True)
                - normed * jnp.mean(dn * normed, axis=-1, keepdims=True)
            )
        ).astype(BF16)
        dact = jnp.einsum("sip,vp->siv", dout, w_2, preferred_element_type=F32)
        sig = jax.nn.sigmoid(pre)
        dpre = (dact * sig * (1.0 + pre * (1.0 - sig))).astype(BF16)
        gnode = gf + jnp.einsum("sip,vp->siv", dpre, w_a, preferred_element_type=F32)
        dagg = jnp.einsum("sip,vp->siv", dpre, w_b, preferred_element_type=F32).astype(BF16)
        spread = jnp.einsum(
            "ij,sid->sjd", adj2, jnp.concatenate([dagg, dagg], axis=1), preferred_element_type=F32
        )
        left_grad = spread[:, :margin].astype(BF16)
        right_grad = spread[:, margin + nb * blk :].astype(BF16)
        own = gnode + spread[:, margin : margin + nb * blk]

        def finish(partial, from_right, from_left):
            blocks = partial.reshape(samples, nb, blk, width)
            blocks = add_blocks(blocks, send_right, hs, from_right)
            blocks = add_blocks(blocks, send_left, hs, from_left)
            return blocks.reshape(samples, node_rows, width).astype(BF16)

        active = sections - 1 - tick
        g_new = finish(
            own,
            lax.ppermute(left_grad, both, route(active, active, -1)),
            lax.ppermute(right_grad, both, route(active, active, 1)),
        )
        if grad_in is None:
            grad_in, dpre_keep, dout_keep = g_new, dpre, dout
            gain_keep = gain_term
        else:
            mine = section_index == active
            grad_in = jnp.where(mine, g_new, grad_in)
            dpre_keep = jnp.where(mine, dpre, dpre_keep)
            dout_keep = jnp.where(mine, dout, dout_keep)
            gain_keep = jnp.where(mine, gain_term, gain_keep)
        if tick + 1 < sections:
            g = finish(
                lax.ppermute(own, both, route(active, active - 1, 0)),
                lax.ppermute(left_grad, both, route(active, active - 1, -1)),
                lax.ppermute(right_grad, both, route(active, active - 1, 1)),
            )

    norm_factor = 1.0 / math.sqrt(samples * node_rows * domains)
    stacked = jnp.concatenate([h_in, agg], axis=2)
    gw1 = jnp.einsum("via,vid->ad", stacked, dpre_keep, preferred_element_type=F32)
    gw2 = jnp.einsum("via,vid->ad", act, dout_keep, preferred_element_type=F32)
    r1 = gw1.shape[0] // domains
    r2 = gw2.shape[0] // domains
    r3 = gain_keep.shape[0] // domains
    pad_rows = 16
    gain_rows = jnp.pad(gain_keep.reshape(domains, 1, r3), ((0, 0), (0, pad_rows - 1), (0, width - r3)))
    packed = jnp.concatenate(
        [
            gw1.reshape(domains, r1, width),
            gw2.reshape(domains, r2, width),
            gain_rows,
        ],
        axis=1,
    ).astype(BF16)
    packed = packed.reshape(domains * (r1 + r2 + pad_rows), width)
    reduced = halving_reduce_scatter(packed, "dom", domains, domain_index)
    reduced = reduced.astype(F32) * norm_factor
    g1 = reduced[:r1]
    g2 = reduced[r1 : r1 + r2]
    g3 = reduced[r1 + r2, :r3]
    return (
        saved_out[None],
        grad_in[None],
        g1[None],
        g2[None],
        g3[None],
    )


def solution(mesh):
    return jax.shard_map(
        shards,
        mesh=mesh,
        in_specs=(
            P("groups", "dom", None),
            P("groups", "dom", None),
            P("section", None, None),
            P("section", None, None),
            P("section", None),
            P("dom", None, None),
            P("dom"),
            P("dom"),
            P("dom"),
            P(),
            P(),
        ),
        out_specs=(
            P("section", "groups", "dom", None),
            P("section", "groups", "dom", None),
            P("section", "dom", "groups"),
            P("section", "dom", "groups"),
            P("section", ("groups", "dom")),
        ),
        check_vma=False,
    )
```

```python
import math

import jax
import jax.numpy as jnp
from jax import lax
from jax.sharding import PartitionSpec as P

EPSILON = 1e-05
HIGHEST_PRECISION = lax.Precision.HIGHEST
F32 = jnp.float32
BF16 = jnp.bfloat16


def pick_blocks(blocks, index, count):
    parts = [lax.dynamic_index_in_dim(blocks, index[i], axis=1, keepdims=False) for i in range(count)]
    return jnp.concatenate(parts, axis=1)


def add_blocks(blocks, index, count, values):
    samples, nb, blk, width = blocks.shape
    values = values.reshape(samples, count, blk, width).astype(F32)
    for i in range(count):
        hit = (jnp.arange(nb) == index[i])[None, :, None, None]
        blocks = blocks + jnp.where(hit, values[:, i][:, None], 0.0)
    return blocks


def halving_reduce_scatter(x, axis, devices, index):
    if devices & (devices - 1):
        return lax.psum_scatter(x, axis, scatter_dimension=0, tiled=True)
    rows = x.shape[0] // devices
    cur = x.reshape(devices, rows, x.shape[1]).astype(F32)
    dist = 1
    while dist < devices:
        cur = cur.reshape(cur.shape[0] // 2, 2, rows, x.shape[1])
        bit = (index // dist) % 2
        low, high = cur[:, 0], cur[:, 1]
        keep = jnp.where(bit == 0, low, high)
        send = jnp.where(bit == 0, high, low).astype(x.dtype)
        pairs = [(i, i ^ dist) for i in range(devices)]
        recv = lax.ppermute(send, axis, pairs)
        cur = keep + recv.astype(F32)
        dist *= 2
    return cur[0]


def shards(
    node_input,
    cotangent,
    w_one,
    w_two,
    gain,
    tile_weights,
    tile_rows,
    tile_cols,
    tile_count,
    halo_from_left,
    halo_from_right,
):
    sections = lax.axis_size("section")
    section_index = lax.axis_index("section")
    domains = lax.axis_size("dom")
    domain_index = lax.axis_index("dom")
    samples, node_rows, width = node_input.shape
    slot_count, blk, _ = tile_weights.shape
    nb = node_rows // blk
    hs = halo_from_left.shape[1]
    ext = nb + 2 * hs
    margin = hs * blk
    offset = domain_index * nb
    send_right = jnp.take(halo_from_left, (domain_index + 1) % domains, axis=0) - offset
    send_left = jnp.take(halo_from_right, (domain_index + domains - 1) % domains, axis=0) - offset

    live = (jnp.arange(slot_count) < tile_count[0]).astype(F32)
    row_oh = (tile_rows[:, None] == jnp.arange(nb)[None, :]).astype(F32) * live[:, None]
    col_oh = (tile_cols[:, None] == jnp.arange(ext)[None, :]).astype(F32)
    pair = (row_oh[:, :, None] * col_oh[:, None, :]).reshape(slot_count, nb * ext)
    adj = jnp.einsum("tp,tij->pij", pair, tile_weights.astype(F32), precision=HIGHEST_PRECISION)
    adj = adj.reshape(nb, ext, blk, blk).transpose(0, 2, 1, 3).reshape(nb * blk, ext * blk)
    adj_hi = adj.astype(BF16)
    adj_lo = (adj - adj_hi.astype(F32)).astype(BF16)
    adj2 = jnp.concatenate([adj_hi, adj_lo], axis=0)

    w_a = w_one[0, :width]
    w_b = w_one[0, width:]
    w_2 = w_two[0]
    gain_row = gain[0]

    both = ("dom", "section")

    def linear(d, s):
        return d * sections + s

    def route(src_section, dst_section, shift):
        return [
            (linear(d, src_section), linear((d + shift) % domains, dst_section))
            for d in range(domains)
        ]

    def forward_layer(h, left, right):
        h_ext = jnp.concatenate([left, h, right], axis=1)
        agg2 = jnp.einsum("ij,sjd->sid", adj2, h_ext, preferred_element_type=F32)
        agg = (agg2[:, : nb * blk] + agg2[:, nb * blk :]).astype(BF16)
        pre = jnp.einsum("sic,ct->sit", h, w_a, preferred_element_type=F32)
        pre = pre + jnp.einsum("sic,ct->sit", agg, w_b, preferred_element_type=F32)
        act = jax.nn.silu(pre).astype(BF16)
        mixed = jnp.einsum("sic,ct->sit", act, w_2, preferred_element_type=F32)
        center = mixed - jnp.mean(mixed, axis=-1, keepdims=True)
        rstd = lax.rsqrt(jnp.mean(center * center, axis=-1, keepdims=True) + EPSILON)
        normed = center * rstd
        out = (h.astype(F32) + normed * gain_row).astype(BF16)
        return out, (h, agg, pre, act, normed, rstd)

    in_blocks = node_input.reshape(samples, nb, blk, width)
    left = lax.ppermute(pick_blocks(in_blocks, send_right, hs), both, route(0, 0, 1))
    right = lax.ppermute(pick_blocks(in_blocks, send_left, hs), both, route(0, 0, -1))
    h = node_input
    saved = None
    saved_out = None
    for tick in range(sections):
        out, res = forward_layer(h, left, right)
        if saved is None:
            saved = res
            saved_out = out
        else:
            mine = section_index == tick
            saved = tuple(jnp.where(mine, a, b) for a, b in zip(res, saved))
            saved_out = jnp.where(mine, out, saved_out)
        if tick + 1 < sections:
            out_blocks = out.reshape(samples, nb, blk, width)
            h = lax.ppermute(out, both, route(tick, tick + 1, 0))
            left = lax.ppermute(pick_blocks(out_blocks, send_right, hs), both, route(tick, tick + 1, 1))
            right = lax.ppermute(pick_blocks(out_blocks, send_left, hs), both, route(tick, tick + 1, -1))

    h_in, agg, pre, act, normed, rstd = saved

    g = cotangent
    grad_in = None
    dpre_keep = None
    dout_keep = None
    gain_keep = None
    for tick in range(sections):
        gf = g.astype(F32)
        gain_term = jnp.sum(gf * normed, axis=(0, 1))
        dn = gf * gain_row
        dout = (
            rstd
            * (
                dn
                - jnp.mean(dn, axis=-1, keepdims=True)
                - normed * jnp.mean(dn * normed, axis=-1, keepdims=True)
            )
        ).astype(BF16)
        dact = jnp.einsum("sip,vp->siv", dout, w_2, preferred_element_type=F32)
        sig = jax.nn.sigmoid(pre)
        dpre = (dact * sig * (1.0 + pre * (1.0 - sig))).astype(BF16)
        gnode = gf + jnp.einsum("sip,vp->siv", dpre, w_a, preferred_element_type=F32)
        dagg = jnp.einsum("sip,vp->siv", dpre, w_b, preferred_element_type=F32).astype(BF16)
        spread = jnp.einsum(
            "ij,sid->sjd", adj2, jnp.concatenate([dagg, dagg], axis=1), preferred_element_type=F32
        )
        left_grad = spread[:, :margin].astype(BF16)
        right_grad = spread[:, margin + nb * blk :].astype(BF16)
        own = gnode + spread[:, margin : margin + nb * blk]

        def finish(partial, from_right, from_left):
            blocks = partial.reshape(samples, nb, blk, width)
            blocks = add_blocks(blocks, send_right, hs, from_right)
            blocks = add_blocks(blocks, send_left, hs, from_left)
            return blocks.reshape(samples, node_rows, width).astype(BF16)

        active = sections - 1 - tick
        mine = section_index == active
        if tick + 1 < sections:
            g = finish(
                lax.ppermute(own, both, route(active, active - 1, 0)),
                lax.ppermute(left_grad, both, route(active, active - 1, -1)),
                lax.ppermute(right_grad, both, route(active, active - 1, 1)),
            )
            g_new = lax.ppermute(g, both, route(active - 1, active, 0))
        else:
            g_new = finish(
                own,
                lax.ppermute(left_grad, both, route(active, active, -1)),
                lax.ppermute(right_grad, both, route(active, active, 1)),
            )
        if grad_in is None:
            grad_in, dpre_keep, dout_keep = g_new, dpre, dout
            gain_keep = gain_term
        else:
            grad_in = jnp.where(mine, g_new, grad_in)
            dpre_keep = jnp.where(mine, dpre, dpre_keep)
            dout_keep = jnp.where(mine, dout, dout_keep)
            gain_keep = jnp.where(mine, gain_term, gain_keep)

    norm_factor = 1.0 / math.sqrt(samples * node_rows * domains)
    stacked = jnp.concatenate([h_in, agg], axis=2)
    gw1 = jnp.einsum("via,vid->ad", stacked, dpre_keep, preferred_element_type=F32)
    gw2 = jnp.einsum("via,vid->ad", act, dout_keep, preferred_element_type=F32)
    r1 = gw1.shape[0] // domains
    r2 = gw2.shape[0] // domains
    r3 = gain_keep.shape[0] // domains
    pad_rows = 16
    gain_rows = jnp.pad(gain_keep.reshape(domains, 1, r3), ((0, 0), (0, pad_rows - 1), (0, width - r3)))
    packed = jnp.concatenate(
        [
            gw1.reshape(domains, r1, width),
            gw2.reshape(domains, r2, width),
            gain_rows,
        ],
        axis=1,
    ).astype(BF16)
    packed = packed.reshape(domains * (r1 + r2 + pad_rows), width)
    reduced = halving_reduce_scatter(packed, "dom", domains, domain_index)
    reduced = reduced.astype(F32) * norm_factor
    g1 = reduced[:r1]
    g2 = reduced[r1 : r1 + r2]
    g3 = reduced[r1 + r2, :r3]
    return (
        saved_out[None],
        grad_in[None],
        g1[None],
        g2[None],
        g3[None],
    )


def solution(mesh):
    return jax.shard_map(
        shards,
        mesh=mesh,
        in_specs=(
            P("groups", "dom", None),
            P("groups", "dom", None),
            P("section", None, None),
            P("section", None, None),
            P("section", None),
            P("dom", None, None),
            P("dom"),
            P("dom"),
            P("dom"),
            P(),
            P(),
        ),
        out_specs=(
            P("section", "groups", "dom", None),
            P("section", "groups", "dom", None),
            P("section", "dom", "groups"),
            P("section", "dom", "groups"),
            P("section", ("groups", "dom")),
        ),
        check_vma=False,
    )
```

```python
import math

import jax
import jax.numpy as jnp
from jax import lax
from jax.sharding import PartitionSpec as P

EPSILON = 1e-05
HIGHEST_PRECISION = lax.Precision.HIGHEST
F32 = jnp.float32
BF16 = jnp.bfloat16


def pick_blocks(blocks, index, count):
    parts = [lax.dynamic_index_in_dim(blocks, index[i], axis=1, keepdims=False) for i in range(count)]
    return jnp.concatenate(parts, axis=1)


def add_blocks(blocks, index, count, values):
    samples, nb, blk, width = blocks.shape
    values = values.reshape(samples, count, blk, width).astype(F32)
    for i in range(count):
        hit = (jnp.arange(nb) == index[i])[None, :, None, None]
        blocks = blocks + jnp.where(hit, values[:, i][:, None], 0.0)
    return blocks


def halving_reduce_scatter(x, axis, devices, index, pairs_of):
    rows = x.shape[0] // devices
    cur = x.reshape(devices, rows, x.shape[1]).astype(F32)
    dist = 1
    while dist < devices:
        cur = cur.reshape(cur.shape[0] // 2, 2, rows, x.shape[1])
        bit = (index // dist) % 2
        low, high = cur[:, 0], cur[:, 1]
        keep = jnp.where(bit == 0, low, high)
        send = jnp.where(bit == 0, high, low).astype(x.dtype)
        recv = lax.ppermute(send, axis, pairs_of(dist))
        cur = keep + recv.astype(F32)
        dist *= 2
    return cur[0]


def shards(
    node_input,
    cotangent,
    w_one,
    w_two,
    gain,
    tile_weights,
    tile_rows,
    tile_cols,
    tile_count,
    halo_from_left,
    halo_from_right,
):
    sections = lax.axis_size("section")
    section_index = lax.axis_index("section")
    domains = lax.axis_size("dom")
    domain_index = lax.axis_index("dom")
    samples, node_rows, width = node_input.shape
    slot_count, blk, _ = tile_weights.shape
    nb = node_rows // blk
    hs = halo_from_left.shape[1]
    ext = nb + 2 * hs
    margin = hs * blk
    offset = domain_index * nb
    send_right = jnp.take(halo_from_left, (domain_index + 1) % domains, axis=0) - offset
    send_left = jnp.take(halo_from_right, (domain_index + domains - 1) % domains, axis=0) - offset

    live = (jnp.arange(slot_count) < tile_count[0]).astype(F32)
    row_oh = (tile_rows[:, None] == jnp.arange(nb)[None, :]).astype(F32) * live[:, None]
    col_oh = (tile_cols[:, None] == jnp.arange(ext)[None, :]).astype(F32)
    pair = (row_oh[:, :, None] * col_oh[:, None, :]).reshape(slot_count, nb * ext)
    adj = jnp.einsum("tp,tij->pij", pair, tile_weights.astype(F32), precision=HIGHEST_PRECISION)
    adj = adj.reshape(nb, ext, blk, blk).transpose(0, 2, 1, 3).reshape(nb * blk, ext * blk)
    adj_hi = adj.astype(BF16)
    adj_lo = (adj - adj_hi.astype(F32)).astype(BF16)
    adj2 = jnp.concatenate([adj_hi, adj_lo], axis=0)

    w_a = w_one[0, :width]
    w_b = w_one[0, width:]
    w_2 = w_two[0]
    gain_row = gain[0]

    both = ("dom", "section")

    def linear(d, s):
        return d * sections + s

    def route(src_section, dst_section, shift):
        return [
            (linear(d, src_section), linear((d + shift) % domains, dst_section))
            for d in range(domains)
        ]

    def forward_layer(h, left, right):
        h_ext = jnp.concatenate([left, h, right], axis=1)
        agg2 = jnp.einsum("ij,sjd->sid", adj2, h_ext, preferred_element_type=F32)
        agg = (agg2[:, : nb * blk] + agg2[:, nb * blk :]).astype(BF16)
        pre = jnp.einsum("sic,ct->sit", h, w_a, preferred_element_type=F32)
        pre = pre + jnp.einsum("sic,ct->sit", agg, w_b, preferred_element_type=F32)
        act = jax.nn.silu(pre).astype(BF16)
        mixed = jnp.einsum("sic,ct->sit", act, w_2, preferred_element_type=F32)
        center = mixed - jnp.mean(mixed, axis=-1, keepdims=True)
        rstd = lax.rsqrt(jnp.mean(center * center, axis=-1, keepdims=True) + EPSILON)
        normed = center * rstd
        out = (h.astype(F32) + normed * gain_row).astype(BF16)
        return out, (h, agg, pre, act, normed, rstd)

    in_blocks = node_input.reshape(samples, nb, blk, width)
    left = lax.ppermute(pick_blocks(in_blocks, send_right, hs), both, route(0, 0, 1))
    right = lax.ppermute(pick_blocks(in_blocks, send_left, hs), both, route(0, 0, -1))
    h = node_input
    saved = None
    saved_out = None
    for tick in range(sections):
        out, res = forward_layer(h, left, right)
        if saved is None:
            saved = res
            saved_out = out
        else:
            mine = section_index == tick
            saved = tuple(jnp.where(mine, a, b) for a, b in zip(res, saved))
            saved_out = jnp.where(mine, out, saved_out)
        if tick + 1 < sections:
            out_blocks = out.reshape(samples, nb, blk, width)
            h = lax.ppermute(out, both, route(tick, tick + 1, 0))
            left = lax.ppermute(pick_blocks(out_blocks, send_right, hs), both, route(tick, tick + 1, 1))
            right = lax.ppermute(pick_blocks(out_blocks, send_left, hs), both, route(tick, tick + 1, -1))

    h_in, agg, pre, act, normed, rstd = saved

    norm_factor = 1.0 / math.sqrt(samples * node_rows * domains)
    stacked = jnp.concatenate([h_in, agg], axis=2)
    r1 = 2 * width // domains
    r2 = width // domains
    r3 = width // domains
    pad_rows = 16
    power_of_two = (domains & (domains - 1)) == 0

    def reduce_grads(dpre, dout, gain_term, active):
        gw1 = jnp.einsum("via,vid->ad", stacked, dpre, preferred_element_type=F32)
        gw2 = jnp.einsum("via,vid->ad", act, dout, preferred_element_type=F32)
        gain_rows = jnp.pad(
            gain_term.reshape(domains, 1, r3), ((0, 0), (0, pad_rows - 1), (0, width - r3))
        )
        packed = jnp.concatenate(
            [gw1.reshape(domains, r1, width), gw2.reshape(domains, r2, width), gain_rows], axis=1
        ).astype(BF16)
        packed = packed.reshape(domains * (r1 + r2 + pad_rows), width)
        if not power_of_two:
            return lax.psum_scatter(packed, "dom", scatter_dimension=0, tiled=True).astype(F32)

        def pairs_of(dist):
            return [(linear(d, active), linear(d ^ dist, active)) for d in range(domains)]

        return halving_reduce_scatter(packed, both, domains, domain_index, pairs_of)

    g = cotangent
    grad_in = None
    reduced = None
    for tick in range(sections):
        gf = g.astype(F32)
        gain_term = jnp.sum(gf * normed, axis=(0, 1))
        dn = gf * gain_row
        dout = (
            rstd
            * (
                dn
                - jnp.mean(dn, axis=-1, keepdims=True)
                - normed * jnp.mean(dn * normed, axis=-1, keepdims=True)
            )
        ).astype(BF16)
        dact = jnp.einsum("sip,vp->siv", dout, w_2, preferred_element_type=F32)
        sig = jax.nn.sigmoid(pre)
        dpre = (dact * sig * (1.0 + pre * (1.0 - sig))).astype(BF16)
        gnode = gf + jnp.einsum("sip,vp->siv", dpre, w_a, preferred_element_type=F32)
        dagg = jnp.einsum("sip,vp->siv", dpre, w_b, preferred_element_type=F32).astype(BF16)
        spread = jnp.einsum(
            "ij,sid->sjd", adj2, jnp.concatenate([dagg, dagg], axis=1), preferred_element_type=F32
        )
        left_grad = spread[:, :margin].astype(BF16)
        right_grad = spread[:, margin + nb * blk :].astype(BF16)
        own = gnode + spread[:, margin : margin + nb * blk]

        def finish(partial, from_right, from_left):
            blocks = partial.reshape(samples, nb, blk, width)
            blocks = add_blocks(blocks, send_right, hs, from_right)
            blocks = add_blocks(blocks, send_left, hs, from_left)
            return blocks.reshape(samples, node_rows, width).astype(BF16)

        active = sections - 1 - tick
        mine = section_index == active
        if tick + 1 < sections:
            g = finish(
                lax.ppermute(own, both, route(active, active - 1, 0)),
                lax.ppermute(left_grad, both, route(active, active - 1, -1)),
                lax.ppermute(right_grad, both, route(active, active - 1, 1)),
            )
            g_new = lax.ppermute(g, both, route(active - 1, active, 0))
        else:
            g_new = finish(
                own,
                lax.ppermute(left_grad, both, route(active, active, -1)),
                lax.ppermute(right_grad, both, route(active, active, 1)),
            )
        reduced_now = reduce_grads(dpre, dout, gain_term, active)
        if grad_in is None:
            grad_in = g_new
            reduced = reduced_now
        else:
            grad_in = jnp.where(mine, g_new, grad_in)
            reduced = jnp.where(mine, reduced_now, reduced)

    reduced = reduced * norm_factor
    g1 = reduced[:r1]
    g2 = reduced[r1 : r1 + r2]
    g3 = reduced[r1 + r2, :r3]
    return (
        saved_out[None],
        grad_in[None],
        g1[None],
        g2[None],
        g3[None],
    )


def solution(mesh):
    return jax.shard_map(
        shards,
        mesh=mesh,
        in_specs=(
            P("groups", "dom", None),
            P("groups", "dom", None),
            P("section", None, None),
            P("section", None, None),
            P("section", None),
            P("dom", None, None),
            P("dom"),
            P("dom"),
            P("dom"),
            P(),
            P(),
        ),
        out_specs=(
            P("section", "groups", "dom", None),
            P("section", "groups", "dom", None),
            P("section", "dom", "groups"),
            P("section", "dom", "groups"),
            P("section", ("groups", "dom")),
        ),
        check_vma=False,
    )
```

```python
import math

import jax
import jax.numpy as jnp
from jax import lax
from jax.sharding import PartitionSpec as P

EPSILON = 1e-05
HIGHEST_PRECISION = lax.Precision.HIGHEST
F32 = jnp.float32
BF16 = jnp.bfloat16


def pick_blocks(blocks, index, count):
    parts = [lax.dynamic_index_in_dim(blocks, index[i], axis=1, keepdims=False) for i in range(count)]
    return jnp.concatenate(parts, axis=1)


def add_blocks(blocks, index, count, values):
    samples, nb, blk, width = blocks.shape
    values = values.reshape(samples, count, blk, width).astype(F32)
    for i in range(count):
        hit = (jnp.arange(nb) == index[i])[None, :, None, None]
        blocks = blocks + jnp.where(hit, values[:, i][:, None], 0.0)
    return blocks


def halving_reduce_scatter(x, axis, devices, index):
    if devices & (devices - 1):
        return lax.psum_scatter(x, axis, scatter_dimension=0, tiled=True)
    rows = x.shape[0] // devices
    cur = x.reshape(devices, rows, x.shape[1]).astype(F32)
    dist = 1
    while dist < devices:
        cur = cur.reshape(cur.shape[0] // 2, 2, rows, x.shape[1])
        bit = (index // dist) % 2
        low, high = cur[:, 0], cur[:, 1]
        keep = jnp.where(bit == 0, low, high)
        send = jnp.where(bit == 0, high, low).astype(x.dtype)
        pairs = [(i, i ^ dist) for i in range(devices)]
        recv = lax.ppermute(send, axis, pairs)
        cur = keep + recv.astype(F32)
        dist *= 2
    return cur[0]


def shards(
    node_input,
    cotangent,
    w_one,
    w_two,
    gain,
    tile_weights,
    tile_rows,
    tile_cols,
    tile_count,
    halo_from_left,
    halo_from_right,
):
    sections = lax.axis_size("section")
    section_index = lax.axis_index("section")
    domains = lax.axis_size("dom")
    domain_index = lax.axis_index("dom")
    samples, node_rows, width = node_input.shape
    slot_count, blk, _ = tile_weights.shape
    nb = node_rows // blk
    hs = halo_from_left.shape[1]
    ext = nb + 2 * hs
    margin = hs * blk
    offset = domain_index * nb
    dom_ids = jnp.arange(domains)[:, None]
    send_right = jnp.sum(jnp.where(dom_ids == (domain_index + 1) % domains, halo_from_left, 0), axis=0) - offset
    send_left = (
        jnp.sum(jnp.where(dom_ids == (domain_index + domains - 1) % domains, halo_from_right, 0), axis=0)
        - offset
    )

    live = (jnp.arange(slot_count) < tile_count[0]).astype(F32)
    row_oh = (tile_rows[:, None] == jnp.arange(nb)[None, :]).astype(F32) * live[:, None]
    col_oh = (tile_cols[:, None] == jnp.arange(ext)[None, :]).astype(F32)
    pair = (row_oh[:, :, None] * col_oh[:, None, :]).reshape(slot_count, nb * ext)
    adj = jnp.einsum("tp,tij->pij", pair, tile_weights.astype(F32), precision=HIGHEST_PRECISION)
    adj = adj.reshape(nb, ext, blk, blk).transpose(0, 2, 1, 3).reshape(nb * blk, ext * blk)
    adj_hi = adj.astype(BF16)
    adj_lo = (adj - adj_hi.astype(F32)).astype(BF16)
    adj2 = jnp.concatenate([adj_hi, adj_lo], axis=0)

    w_a = w_one[0, :width]
    w_b = w_one[0, width:]
    w_2 = w_two[0]
    gain_row = gain[0]

    both = ("dom", "section")

    def linear(d, s):
        return d * sections + s

    def route(src_section, dst_section, shift):
        return [
            (linear(d, src_section), linear((d + shift) % domains, dst_section))
            for d in range(domains)
        ]

    def forward_layer(h, left, right):
        h_ext = jnp.concatenate([left, h, right], axis=1)
        agg2 = jnp.einsum("ij,sjd->sid", adj2, h_ext, preferred_element_type=F32)
        agg = (agg2[:, : nb * blk] + agg2[:, nb * blk :]).astype(BF16)
        pre = jnp.einsum("sic,ct->sit", h, w_a, preferred_element_type=F32)
        pre = pre + jnp.einsum("sic,ct->sit", agg, w_b, preferred_element_type=F32)
        act = jax.nn.silu(pre).astype(BF16)
        mixed = jnp.einsum("sic,ct->sit", act, w_2, preferred_element_type=F32)
        center = mixed - jnp.mean(mixed, axis=-1, keepdims=True)
        rstd = lax.rsqrt(jnp.mean(center * center, axis=-1, keepdims=True) + EPSILON)
        normed = center * rstd
        out = (h.astype(F32) + normed * gain_row).astype(BF16)
        return out, (h, agg, pre, act, normed, rstd)

    in_blocks = node_input.reshape(samples, nb, blk, width)
    left = lax.ppermute(pick_blocks(in_blocks, send_right, hs), both, route(0, 0, 1))
    right = lax.ppermute(pick_blocks(in_blocks, send_left, hs), both, route(0, 0, -1))
    h = node_input
    saved = None
    saved_out = None
    last_res = None
    for tick in range(sections):
        out, res = forward_layer(h, left, right)
        last_res = res
        if saved is None:
            saved = res
            saved_out = out
        else:
            mine = section_index == tick
            saved = tuple(jnp.where(mine, a, b) for a, b in zip(res, saved))
            saved_out = jnp.where(mine, out, saved_out)
        if tick + 1 < sections:
            out_blocks = out.reshape(samples, nb, blk, width)
            h = lax.ppermute(out, both, route(tick, tick + 1, 0))
            left = lax.ppermute(pick_blocks(out_blocks, send_right, hs), both, route(tick, tick + 1, 1))
            right = lax.ppermute(pick_blocks(out_blocks, send_left, hs), both, route(tick, tick + 1, -1))

    h_in, agg, pre, act, normed, rstd = saved
    _, _, pre_last, _, normed_last, rstd_last = last_res

    g = cotangent
    grad_in = None
    dpre_keep = None
    dout_keep = None
    gain_keep = None
    for tick in range(sections):
        if tick == 0:
            pre_t, normed_t, rstd_t = pre_last, normed_last, rstd_last
        else:
            pre_t, normed_t, rstd_t = pre, normed, rstd
        gf = g.astype(F32)
        gain_term = jnp.sum(gf * normed_t, axis=(0, 1))
        dn = gf * gain_row
        dout = (
            rstd_t
            * (
                dn
                - jnp.mean(dn, axis=-1, keepdims=True)
                - normed_t * jnp.mean(dn * normed_t, axis=-1, keepdims=True)
            )
        ).astype(BF16)
        dact = jnp.einsum("sip,vp->siv", dout, w_2, preferred_element_type=F32)
        sig = jax.nn.sigmoid(pre_t)
        dpre = (dact * sig * (1.0 + pre_t * (1.0 - sig))).astype(BF16)
        gnode = gf + jnp.einsum("sip,vp->siv", dpre, w_a, preferred_element_type=F32)
        dagg = jnp.einsum("sip,vp->siv", dpre, w_b, preferred_element_type=F32).astype(BF16)
        spread = jnp.einsum(
            "ij,sid->sjd", adj2, jnp.concatenate([dagg, dagg], axis=1), preferred_element_type=F32
        )
        left_grad = spread[:, :margin].astype(BF16)
        right_grad = spread[:, margin + nb * blk :].astype(BF16)
        own = gnode + spread[:, margin : margin + nb * blk]

        def finish(partial, from_right, from_left):
            blocks = partial.reshape(samples, nb, blk, width)
            blocks = add_blocks(blocks, send_right, hs, from_right)
            blocks = add_blocks(blocks, send_left, hs, from_left)
            return blocks.reshape(samples, node_rows, width).astype(BF16)

        active = sections - 1 - tick
        mine = section_index == active
        if tick + 1 < sections:
            g = finish(
                lax.ppermute(own, both, route(active, active - 1, 0)),
                lax.ppermute(left_grad, both, route(active, active - 1, -1)),
                lax.ppermute(right_grad, both, route(active, active - 1, 1)),
            )
            g_new = lax.ppermute(g, both, route(active - 1, active, 0))
        else:
            g_new = finish(
                own,
                lax.ppermute(left_grad, both, route(active, active, -1)),
                lax.ppermute(right_grad, both, route(active, active, 1)),
            )
        if grad_in is None:
            grad_in, dpre_keep, dout_keep = g_new, dpre, dout
            gain_keep = gain_term
        else:
            grad_in = jnp.where(mine, g_new, grad_in)
            dpre_keep = jnp.where(mine, dpre, dpre_keep)
            dout_keep = jnp.where(mine, dout, dout_keep)
            gain_keep = jnp.where(mine, gain_term, gain_keep)

    norm_factor = 1.0 / math.sqrt(samples * node_rows * domains)
    stacked = jnp.concatenate([h_in, agg], axis=2)
    gw1 = jnp.einsum("via,vid->ad", stacked, dpre_keep, preferred_element_type=F32)
    gw2 = jnp.einsum("via,vid->ad", act, dout_keep, preferred_element_type=F32)
    r1 = gw1.shape[0] // domains
    r2 = gw2.shape[0] // domains
    r3 = gain_keep.shape[0] // domains
    pad_rows = 16
    gain_rows = jnp.pad(gain_keep.reshape(domains, 1, r3), ((0, 0), (0, pad_rows - 1), (0, width - r3)))
    packed = jnp.concatenate(
        [
            gw1.reshape(domains, r1, width),
            gw2.reshape(domains, r2, width),
            gain_rows,
        ],
        axis=1,
    ).astype(BF16)
    packed = packed.reshape(domains * (r1 + r2 + pad_rows), width)
    reduced = halving_reduce_scatter(packed, "dom", domains, domain_index)
    reduced = reduced.astype(F32) * norm_factor
    g1 = reduced[:r1]
    g2 = reduced[r1 : r1 + r2]
    g3 = reduced[r1 + r2, :r3]
    return (
        saved_out[None],
        grad_in[None],
        g1[None],
        g2[None],
        g3[None],
    )


def solution(mesh):
    return jax.shard_map(
        shards,
        mesh=mesh,
        in_specs=(
            P("groups", "dom", None),
            P("groups", "dom", None),
            P("section", None, None),
            P("section", None, None),
            P("section", None),
            P("dom", None, None),
            P("dom"),
            P("dom"),
            P("dom"),
            P(),
            P(),
        ),
        out_specs=(
            P("section", "groups", "dom", None),
            P("section", "groups", "dom", None),
            P("section", "dom", "groups"),
            P("section", "dom", "groups"),
            P("section", ("groups", "dom")),
        ),
        check_vma=False,
    )
```

```python
import math

import jax
import jax.numpy as jnp
from jax import lax
from jax.sharding import PartitionSpec as P

EPSILON = 1e-05
HIGHEST_PRECISION = lax.Precision.HIGHEST
F32 = jnp.float32
BF16 = jnp.bfloat16


def pick_blocks(blocks, index, count):
    parts = [lax.dynamic_index_in_dim(blocks, index[i], axis=1, keepdims=False) for i in range(count)]
    return jnp.concatenate(parts, axis=1)


def add_blocks(blocks, index, count, values):
    samples, nb, blk, width = blocks.shape
    values = values.reshape(samples, count, blk, width).astype(F32)
    for i in range(count):
        hit = (jnp.arange(nb) == index[i])[None, :, None, None]
        blocks = blocks + jnp.where(hit, values[:, i][:, None], 0.0)
    return blocks


def halving_reduce_scatter(x, axis, devices, index):
    if devices & (devices - 1):
        return lax.psum_scatter(x, axis, scatter_dimension=0, tiled=True)
    rows = x.shape[0] // devices
    cur = x.reshape(devices, rows, x.shape[1]).astype(F32)
    dist = 1
    while dist < devices:
        cur = cur.reshape(cur.shape[0] // 2, 2, rows, x.shape[1])
        bit = (index // dist) % 2
        low, high = cur[:, 0], cur[:, 1]
        keep = jnp.where(bit == 0, low, high)
        send = jnp.where(bit == 0, high, low).astype(x.dtype)
        pairs = [(i, i ^ dist) for i in range(devices)]
        recv = lax.ppermute(send, axis, pairs)
        cur = keep + recv.astype(F32)
        dist *= 2
    return cur[0]


def shards(
    node_input,
    cotangent,
    w_one,
    w_two,
    gain,
    tile_weights,
    tile_rows,
    tile_cols,
    tile_count,
    halo_from_left,
    halo_from_right,
):
    sections = lax.axis_size("section")
    section_index = lax.axis_index("section")
    domains = lax.axis_size("dom")
    domain_index = lax.axis_index("dom")
    samples, node_rows, width = node_input.shape
    slot_count, blk, _ = tile_weights.shape
    nb = node_rows // blk
    hs = halo_from_left.shape[1]
    ext = nb + 2 * hs
    margin = hs * blk
    offset = domain_index * nb
    dom_ids = jnp.arange(domains)[:, None]
    send_right = jnp.sum(jnp.where(dom_ids == (domain_index + 1) % domains, halo_from_left, 0), axis=0) - offset
    send_left = (
        jnp.sum(jnp.where(dom_ids == (domain_index + domains - 1) % domains, halo_from_right, 0), axis=0)
        - offset
    )

    live = (jnp.arange(slot_count) < tile_count[0]).astype(F32)
    row_oh = (tile_rows[:, None] == jnp.arange(nb)[None, :]).astype(F32) * live[:, None]
    col_oh = (tile_cols[:, None] == jnp.arange(ext)[None, :]).astype(F32)
    pair = (row_oh[:, :, None] * col_oh[:, None, :]).reshape(slot_count, nb * ext)
    adj = jnp.einsum("tp,tij->pij", pair, tile_weights.astype(F32), precision=HIGHEST_PRECISION)
    adj = adj.reshape(nb, ext, blk, blk).transpose(0, 2, 1, 3).reshape(nb * blk, ext * blk)
    adj_hi = adj.astype(BF16)
    adj_lo = (adj - adj_hi.astype(F32)).astype(BF16)
    adj2 = jnp.concatenate([adj_hi, adj_lo], axis=0)

    w_a = w_one[0, :width]
    w_b = w_one[0, width:]
    w_2 = w_two[0]
    gain_row = gain[0]

    both = ("dom", "section")

    def linear(d, s):
        return d * sections + s

    def route(src_section, dst_section, shift):
        return [
            (linear(d, src_section), linear((d + shift) % domains, dst_section))
            for d in range(domains)
        ]

    def forward_layer(h, left, right):
        h_ext = jnp.concatenate([left, h, right], axis=1)
        agg2 = jnp.einsum("ij,sjd->sid", adj2, h_ext, preferred_element_type=F32)
        agg = (agg2[:, : nb * blk] + agg2[:, nb * blk :]).astype(BF16)
        pre = jnp.einsum("sic,ct->sit", h, w_a, preferred_element_type=F32)
        pre = pre + jnp.einsum("sic,ct->sit", agg, w_b, preferred_element_type=F32)
        act = jax.nn.silu(pre).astype(BF16)
        mixed = jnp.einsum("sic,ct->sit", act, w_2, preferred_element_type=F32)
        center = mixed - jnp.mean(mixed, axis=-1, keepdims=True)
        rstd = lax.rsqrt(jnp.mean(center * center, axis=-1, keepdims=True) + EPSILON)
        normed = center * rstd
        out = (h.astype(F32) + normed * gain_row).astype(BF16)
        return out, (h, agg, pre, act, normed, rstd)

    in_blocks = node_input.reshape(samples, nb, blk, width)
    left = lax.ppermute(pick_blocks(in_blocks, send_right, hs), both, route(0, 0, 1))
    right = lax.ppermute(pick_blocks(in_blocks, send_left, hs), both, route(0, 0, -1))
    h = node_input
    saved = None
    saved_out = None
    last_res = None
    for tick in range(sections):
        out, res = forward_layer(h, left, right)
        last_res = res
        if saved is None:
            saved = res
            saved_out = out
        else:
            mine = section_index == tick
            saved = tuple(jnp.where(mine, a, b) for a, b in zip(res, saved))
            saved_out = jnp.where(mine, out, saved_out)
        if tick + 1 < sections:
            out_blocks = out.reshape(samples, nb, blk, width)
            h = lax.ppermute(out, both, route(tick, tick + 1, 0))
            left = lax.ppermute(pick_blocks(out_blocks, send_right, hs), both, route(tick, tick + 1, 1))
            right = lax.ppermute(pick_blocks(out_blocks, send_left, hs), both, route(tick, tick + 1, -1))

    h_in, agg, pre, act, normed, rstd = saved
    _, _, pre_last, _, normed_last, rstd_last = last_res

    g = cotangent
    grad_in = None
    dpre_keep = None
    dout_keep = None
    gain_keep = None
    for tick in range(sections):
        if tick == 0:
            pre_t, normed_t, rstd_t = pre_last, normed_last, rstd_last
        else:
            pre_t, normed_t, rstd_t = pre, normed, rstd
        gf = g.astype(F32)
        gain_term = jnp.sum(gf * normed_t, axis=(0, 1))
        dn = gf * gain_row
        dout = (
            rstd_t
            * (
                dn
                - jnp.mean(dn, axis=-1, keepdims=True)
                - normed_t * jnp.mean(dn * normed_t, axis=-1, keepdims=True)
            )
        ).astype(BF16)
        dact = jnp.einsum("sip,vp->siv", dout, w_2, preferred_element_type=F32)
        sig = jax.nn.sigmoid(pre_t)
        dpre = (dact * sig * (1.0 + pre_t * (1.0 - sig))).astype(BF16)
        gnode = gf + jnp.einsum("sip,vp->siv", dpre, w_a, preferred_element_type=F32)
        dagg = jnp.einsum("sip,vp->siv", dpre, w_b, preferred_element_type=F32).astype(BF16)
        spread = jnp.einsum(
            "ij,sid->sjd", adj2, jnp.concatenate([dagg, dagg], axis=1), preferred_element_type=F32
        )
        left_grad = spread[:, :margin].astype(BF16)
        right_grad = spread[:, margin + nb * blk :].astype(BF16)
        own = gnode + spread[:, margin : margin + nb * blk]

        def finish(partial, from_right, from_left):
            blocks = partial.reshape(samples, nb, blk, width)
            blocks = add_blocks(blocks, send_right, hs, from_right)
            blocks = add_blocks(blocks, send_left, hs, from_left)
            return blocks.reshape(samples, node_rows, width).astype(BF16)

        active = sections - 1 - tick
        mine = section_index == active
        if tick + 1 < sections:
            g = finish(
                lax.ppermute(own.astype(BF16), both, route(active, active - 1, 0)),
                lax.ppermute(left_grad, both, route(active, active - 1, -1)),
                lax.ppermute(right_grad, both, route(active, active - 1, 1)),
            )
            g_new = lax.ppermute(g, both, route(active - 1, active, 0))
        else:
            g_new = finish(
                own,
                lax.ppermute(left_grad, both, route(active, active, -1)),
                lax.ppermute(right_grad, both, route(active, active, 1)),
            )
        if grad_in is None:
            grad_in, dpre_keep, dout_keep = g_new, dpre, dout
            gain_keep = gain_term
        else:
            grad_in = jnp.where(mine, g_new, grad_in)
            dpre_keep = jnp.where(mine, dpre, dpre_keep)
            dout_keep = jnp.where(mine, dout, dout_keep)
            gain_keep = jnp.where(mine, gain_term, gain_keep)

    norm_factor = 1.0 / math.sqrt(samples * node_rows * domains)
    stacked = jnp.concatenate([h_in, agg], axis=2)
    gw1 = jnp.einsum("via,vid->ad", stacked, dpre_keep, preferred_element_type=F32)
    gw2 = jnp.einsum("via,vid->ad", act, dout_keep, preferred_element_type=F32)
    r1 = gw1.shape[0] // domains
    r2 = gw2.shape[0] // domains
    r3 = gain_keep.shape[0] // domains
    pad_rows = 16
    gain_rows = jnp.pad(gain_keep.reshape(domains, 1, r3), ((0, 0), (0, pad_rows - 1), (0, width - r3)))
    packed = jnp.concatenate(
        [
            gw1.reshape(domains, r1, width),
            gw2.reshape(domains, r2, width),
            gain_rows,
        ],
        axis=1,
    ).astype(BF16)
    packed = packed.reshape(domains * (r1 + r2 + pad_rows), width)
    reduced = halving_reduce_scatter(packed, "dom", domains, domain_index)
    reduced = reduced.astype(F32) * norm_factor
    g1 = reduced[:r1]
    g2 = reduced[r1 : r1 + r2]
    g3 = reduced[r1 + r2, :r3]
    return (
        saved_out[None],
        grad_in[None],
        g1[None],
        g2[None],
        g3[None],
    )


def solution(mesh):
    return jax.shard_map(
        shards,
        mesh=mesh,
        in_specs=(
            P("groups", "dom", None),
            P("groups", "dom", None),
            P("section", None, None),
            P("section", None, None),
            P("section", None),
            P("dom", None, None),
            P("dom"),
            P("dom"),
            P("dom"),
            P(),
            P(),
        ),
        out_specs=(
            P("section", "groups", "dom", None),
            P("section", "groups", "dom", None),
            P("section", "dom", "groups"),
            P("section", "dom", "groups"),
            P("section", ("groups", "dom")),
        ),
        check_vma=False,
    )
```

```python
import math

import jax
import jax.numpy as jnp
from jax import lax
from jax.sharding import PartitionSpec as P

EPSILON = 1e-05
HIGHEST_PRECISION = lax.Precision.HIGHEST
F32 = jnp.float32
BF16 = jnp.bfloat16


def pick_blocks(blocks, index, count):
    parts = [lax.dynamic_index_in_dim(blocks, index[i], axis=1, keepdims=False) for i in range(count)]
    return jnp.concatenate(parts, axis=1)


def add_blocks(blocks, index, count, values):
    samples, nb, blk, width = blocks.shape
    values = values.reshape(samples, count, blk, width).astype(F32)
    for i in range(count):
        hit = (jnp.arange(nb) == index[i])[None, :, None, None]
        blocks = blocks + jnp.where(hit, values[:, i][:, None], 0.0)
    return blocks


def halving_reduce_scatter(x, axis, devices, index, pairs_of):
    rows = x.shape[0] // devices
    cur = x.reshape(devices, rows, x.shape[1]).astype(F32)
    dist = 1
    while dist < devices:
        cur = cur.reshape(cur.shape[0] // 2, 2, rows, x.shape[1])
        bit = (index // dist) % 2
        low, high = cur[:, 0], cur[:, 1]
        keep = jnp.where(bit == 0, low, high)
        send = jnp.where(bit == 0, high, low).astype(x.dtype)
        recv = lax.ppermute(send, axis, pairs_of(dist))
        cur = keep + recv.astype(F32)
        dist *= 2
    return cur[0]


def shards(
    node_input,
    cotangent,
    w_one,
    w_two,
    gain,
    tile_weights,
    tile_rows,
    tile_cols,
    tile_count,
    halo_from_left,
    halo_from_right,
):
    sections = lax.axis_size("section")
    section_index = lax.axis_index("section")
    domains = lax.axis_size("dom")
    domain_index = lax.axis_index("dom")
    samples, node_rows, width = node_input.shape
    slot_count, blk, _ = tile_weights.shape
    nb = node_rows // blk
    hs = halo_from_left.shape[1]
    ext = nb + 2 * hs
    margin = hs * blk
    offset = domain_index * nb
    dom_ids = jnp.arange(domains)[:, None]
    send_right = jnp.sum(jnp.where(dom_ids == (domain_index + 1) % domains, halo_from_left, 0), axis=0) - offset
    send_left = (
        jnp.sum(jnp.where(dom_ids == (domain_index + domains - 1) % domains, halo_from_right, 0), axis=0)
        - offset
    )

    live = (jnp.arange(slot_count) < tile_count[0]).astype(F32)
    row_oh = (tile_rows[:, None] == jnp.arange(nb)[None, :]).astype(F32) * live[:, None]
    col_oh = (tile_cols[:, None] == jnp.arange(ext)[None, :]).astype(F32)
    pair = (row_oh[:, :, None] * col_oh[:, None, :]).reshape(slot_count, nb * ext)
    adj = jnp.einsum("tp,tij->pij", pair, tile_weights.astype(F32), precision=HIGHEST_PRECISION)
    adj = adj.reshape(nb, ext, blk, blk).transpose(0, 2, 1, 3).reshape(nb * blk, ext * blk)
    adj_hi = adj.astype(BF16)
    adj_lo = (adj - adj_hi.astype(F32)).astype(BF16)
    adj2 = jnp.concatenate([adj_hi, adj_lo], axis=0)

    w_a = w_one[0, :width]
    w_b = w_one[0, width:]
    w_2 = w_two[0]
    gain_row = gain[0]

    both = ("dom", "section")

    def linear(d, s):
        return d * sections + s

    def route(src_section, dst_section, shift):
        return [
            (linear(d, src_section), linear((d + shift) % domains, dst_section))
            for d in range(domains)
        ]

    def forward_layer(h, left, right):
        h_ext = jnp.concatenate([left, h, right], axis=1)
        agg2 = jnp.einsum("ij,sjd->sid", adj2, h_ext, preferred_element_type=F32)
        agg = (agg2[:, : nb * blk] + agg2[:, nb * blk :]).astype(BF16)
        pre = jnp.einsum("sic,ct->sit", h, w_a, preferred_element_type=F32)
        pre = pre + jnp.einsum("sic,ct->sit", agg, w_b, preferred_element_type=F32)
        act = jax.nn.silu(pre).astype(BF16)
        mixed = jnp.einsum("sic,ct->sit", act, w_2, preferred_element_type=F32)
        center = mixed - jnp.mean(mixed, axis=-1, keepdims=True)
        rstd = lax.rsqrt(jnp.mean(center * center, axis=-1, keepdims=True) + EPSILON)
        normed = center * rstd
        out = (h.astype(F32) + normed * gain_row).astype(BF16)
        return out, (h, agg, pre, act, normed, rstd)

    in_blocks = node_input.reshape(samples, nb, blk, width)
    left = lax.ppermute(pick_blocks(in_blocks, send_right, hs), both, route(0, 0, 1))
    right = lax.ppermute(pick_blocks(in_blocks, send_left, hs), both, route(0, 0, -1))
    h = node_input
    saved = None
    saved_out = None
    last_res = None
    for tick in range(sections):
        out, res = forward_layer(h, left, right)
        last_res = res
        if saved is None:
            saved = res
            saved_out = out
        else:
            mine = section_index == tick
            saved = tuple(jnp.where(mine, a, b) for a, b in zip(res, saved))
            saved_out = jnp.where(mine, out, saved_out)
        if tick + 1 < sections:
            out_blocks = out.reshape(samples, nb, blk, width)
            h = lax.ppermute(out, both, route(tick, tick + 1, 0))
            left = lax.ppermute(pick_blocks(out_blocks, send_right, hs), both, route(tick, tick + 1, 1))
            right = lax.ppermute(pick_blocks(out_blocks, send_left, hs), both, route(tick, tick + 1, -1))

    h_in, agg, pre, act, normed, rstd = saved
    _, _, pre_last, _, normed_last, rstd_last = last_res

    norm_factor = 1.0 / math.sqrt(samples * node_rows * domains)
    stacked = jnp.concatenate([h_in, agg], axis=2)
    r1 = 2 * width // domains
    r2 = width // domains
    r3 = width // domains
    pad_rows = 16

    def reduce_sections(dpre_s, dout_s, gain_s, members):
        gw1 = jnp.einsum("via,vid->ad", stacked, dpre_s, preferred_element_type=F32)
        gw2 = jnp.einsum("via,vid->ad", act, dout_s, preferred_element_type=F32)
        gain_rows = jnp.pad(gain_s.reshape(domains, 1, r3), ((0, 0), (0, pad_rows - 1), (0, width - r3)))
        packed = jnp.concatenate(
            [gw1.reshape(domains, r1, width), gw2.reshape(domains, r2, width), gain_rows], axis=1
        ).astype(BF16)
        packed = packed.reshape(domains * (r1 + r2 + pad_rows), width)
        if domains & (domains - 1):
            return lax.psum_scatter(packed, "dom", scatter_dimension=0, tiled=True).astype(F32)

        def pairs_of(dist):
            return [(linear(d, s), linear(d ^ dist, s)) for d in range(domains) for s in members]

        return halving_reduce_scatter(packed, both, domains, domain_index, pairs_of)

    g = cotangent
    grad_in = None
    dpre_keep = None
    dout_keep = None
    gain_keep = None
    for tick in range(sections):
        if tick == 0:
            pre_t, normed_t, rstd_t = pre_last, normed_last, rstd_last
        else:
            pre_t, normed_t, rstd_t = pre, normed, rstd
        gf = g.astype(F32)
        gain_term = jnp.sum(gf * normed_t, axis=(0, 1))
        dn = gf * gain_row
        dout = (
            rstd_t
            * (
                dn
                - jnp.mean(dn, axis=-1, keepdims=True)
                - normed_t * jnp.mean(dn * normed_t, axis=-1, keepdims=True)
            )
        ).astype(BF16)
        dact = jnp.einsum("sip,vp->siv", dout, w_2, preferred_element_type=F32)
        sig = jax.nn.sigmoid(pre_t)
        dpre = (dact * sig * (1.0 + pre_t * (1.0 - sig))).astype(BF16)
        gnode = gf + jnp.einsum("sip,vp->siv", dpre, w_a, preferred_element_type=F32)
        dagg = jnp.einsum("sip,vp->siv", dpre, w_b, preferred_element_type=F32).astype(BF16)
        spread = jnp.einsum(
            "ij,sid->sjd", adj2, jnp.concatenate([dagg, dagg], axis=1), preferred_element_type=F32
        )
        left_grad = spread[:, :margin].astype(BF16)
        right_grad = spread[:, margin + nb * blk :].astype(BF16)
        own = gnode + spread[:, margin : margin + nb * blk]

        def finish(partial, from_right, from_left):
            blocks = partial.reshape(samples, nb, blk, width)
            blocks = add_blocks(blocks, send_right, hs, from_right)
            blocks = add_blocks(blocks, send_left, hs, from_left)
            return blocks.reshape(samples, node_rows, width).astype(BF16)

        active = sections - 1 - tick
        mine = section_index == active
        if tick + 1 < sections:
            g = finish(
                lax.ppermute(own.astype(BF16), both, route(active, active - 1, 0)),
                lax.ppermute(left_grad, both, route(active, active - 1, -1)),
                lax.ppermute(right_grad, both, route(active, active - 1, 1)),
            )
            g_new = lax.ppermute(g, both, route(active - 1, active, 0))
        else:
            g_new = finish(
                own,
                lax.ppermute(left_grad, both, route(active, active, -1)),
                lax.ppermute(right_grad, both, route(active, active, 1)),
            )
        if grad_in is None:
            grad_in, dpre_keep, dout_keep = g_new, dpre, dout
            gain_keep = gain_term
        else:
            grad_in = jnp.where(mine, g_new, grad_in)
            dpre_keep = jnp.where(mine, dpre, dpre_keep)
            dout_keep = jnp.where(mine, dout, dout_keep)
            gain_keep = jnp.where(mine, gain_term, gain_keep)
        if tick == sections - 2:
            early = reduce_sections(dpre_keep, dout_keep, gain_keep, tuple(range(1, sections)))

    reduced = reduce_sections(dpre, dout, gain_term, (0,))
    if early is not None:
        reduced = jnp.where(section_index == 0, reduced, early)
    reduced = reduced * norm_factor
    g1 = reduced[:r1]
    g2 = reduced[r1 : r1 + r2]
    g3 = reduced[r1 + r2, :r3]
    return (
        saved_out[None],
        grad_in[None],
        g1[None],
        g2[None],
        g3[None],
    )


def solution(mesh):
    return jax.shard_map(
        shards,
        mesh=mesh,
        in_specs=(
            P("groups", "dom", None),
            P("groups", "dom", None),
            P("section", None, None),
            P("section", None, None),
            P("section", None),
            P("dom", None, None),
            P("dom"),
            P("dom"),
            P("dom"),
            P(),
            P(),
        ),
        out_specs=(
            P("section", "groups", "dom", None),
            P("section", "groups", "dom", None),
            P("section", "dom", "groups"),
            P("section", "dom", "groups"),
            P("section", ("groups", "dom")),
        ),
        check_vma=False,
    )
```

```python
import math

import jax
import jax.numpy as jnp
from jax import lax
from jax.sharding import PartitionSpec as P

EPSILON = 1e-05
HIGHEST_PRECISION = lax.Precision.HIGHEST
F32 = jnp.float32
BF16 = jnp.bfloat16


def pick_blocks(blocks, index, count):
    parts = [lax.dynamic_index_in_dim(blocks, index[i], axis=1, keepdims=False) for i in range(count)]
    return jnp.concatenate(parts, axis=1)


def add_blocks(blocks, index, count, values):
    samples, nb, blk, width = blocks.shape
    values = values.reshape(samples, count, blk, width).astype(F32)
    for i in range(count):
        hit = (jnp.arange(nb) == index[i])[None, :, None, None]
        blocks = blocks + jnp.where(hit, values[:, i][:, None], 0.0)
    return blocks


def halving_reduce_scatter(x, axis, devices, index):
    if devices & (devices - 1):
        return lax.psum_scatter(x, axis, scatter_dimension=0, tiled=True)
    rows = x.shape[0] // devices
    cur = x.reshape(devices, rows, x.shape[1]).astype(F32)
    dist = 1
    while dist < devices:
        cur = cur.reshape(cur.shape[0] // 2, 2, rows, x.shape[1])
        bit = (index // dist) % 2
        low, high = cur[:, 0], cur[:, 1]
        keep = jnp.where(bit == 0, low, high)
        send = jnp.where(bit == 0, high, low).astype(x.dtype)
        pairs = [(i, i ^ dist) for i in range(devices)]
        recv = lax.ppermute(send, axis, pairs)
        cur = keep + recv.astype(F32)
        dist *= 2
    return cur[0]


def shards(
    node_input,
    cotangent,
    w_one,
    w_two,
    gain,
    tile_weights,
    tile_rows,
    tile_cols,
    tile_count,
    halo_from_left,
    halo_from_right,
):
    sections = lax.axis_size("section")
    section_index = lax.axis_index("section")
    domains = lax.axis_size("dom")
    domain_index = lax.axis_index("dom")
    samples, node_rows, width = node_input.shape
    slot_count, blk, _ = tile_weights.shape
    nb = node_rows // blk
    hs = halo_from_left.shape[1]
    ext = nb + 2 * hs
    margin = hs * blk
    offset = domain_index * nb
    dom_ids = jnp.arange(domains)[:, None]
    send_right = jnp.sum(jnp.where(dom_ids == (domain_index + 1) % domains, halo_from_left, 0), axis=0) - offset
    send_left = (
        jnp.sum(jnp.where(dom_ids == (domain_index + domains - 1) % domains, halo_from_right, 0), axis=0)
        - offset
    )

    live = (jnp.arange(slot_count) < tile_count[0]).astype(F32)
    row_oh = (tile_rows[:, None] == jnp.arange(nb)[None, :]).astype(F32) * live[:, None]
    col_oh = (tile_cols[:, None] == jnp.arange(ext)[None, :]).astype(F32)
    pair = (row_oh[:, :, None] * col_oh[:, None, :]).reshape(slot_count, nb * ext)
    adj = jnp.einsum("tp,tij->pij", pair, tile_weights.astype(F32), precision=HIGHEST_PRECISION)
    adj = adj.reshape(nb, ext, blk, blk).transpose(0, 2, 1, 3).reshape(nb * blk, ext * blk)
    adj_hi = adj.astype(BF16)
    adj_lo = (adj - adj_hi.astype(F32)).astype(BF16)
    adj2 = jnp.concatenate([adj_hi, adj_lo], axis=0)

    w_a = w_one[0, :width]
    w_b = w_one[0, width:]
    w_2 = w_two[0]
    gain_row = gain[0]

    both = ("dom", "section")

    def linear(d, s):
        return d * sections + s

    def route(src_section, dst_section, shift):
        return [
            (linear(d, src_section), linear((d + shift) % domains, dst_section))
            for d in range(domains)
        ]

    def forward_layer(h, left, right):
        h_ext = jnp.concatenate([left, h, right], axis=1)
        agg2 = jnp.einsum("ij,sjd->sid", adj2, h_ext, preferred_element_type=F32)
        agg = (agg2[:, : nb * blk] + agg2[:, nb * blk :]).astype(BF16)
        pre = jnp.einsum("sic,ct->sit", h, w_a, preferred_element_type=F32)
        pre = pre + jnp.einsum("sic,ct->sit", agg, w_b, preferred_element_type=F32)
        act = jax.nn.silu(pre).astype(BF16)
        mixed = jnp.einsum("sic,ct->sit", act, w_2, preferred_element_type=F32)
        center = mixed - jnp.mean(mixed, axis=-1, keepdims=True)
        rstd = lax.rsqrt(jnp.mean(center * center, axis=-1, keepdims=True) + EPSILON)
        normed = center * rstd
        out = (h.astype(F32) + normed * gain_row).astype(BF16)
        return out, (h, agg, pre, act, normed, rstd)

    in_blocks = node_input.reshape(samples, nb, blk, width)
    left = lax.ppermute(pick_blocks(in_blocks, send_right, hs), both, route(0, 0, 1))
    right = lax.ppermute(pick_blocks(in_blocks, send_left, hs), both, route(0, 0, -1))
    h = node_input
    saved = None
    saved_out = None
    last_res = None
    for tick in range(sections):
        out, res = forward_layer(h, left, right)
        last_res = res
        last_out = out
        if saved is None:
            saved = res
            saved_out = out
        elif tick + 1 < sections:
            mine = section_index == tick
            saved = tuple(jnp.where(mine, a, b) for a, b in zip(res, saved))
            saved_out = jnp.where(mine, out, saved_out)
        if tick + 1 < sections:
            out_blocks = out.reshape(samples, nb, blk, width)
            h = lax.ppermute(out, both, route(tick, tick + 1, 0))
            left = lax.ppermute(pick_blocks(out_blocks, send_right, hs), both, route(tick, tick + 1, 1))
            right = lax.ppermute(pick_blocks(out_blocks, send_left, hs), both, route(tick, tick + 1, -1))

    _, _, pre, _, normed, rstd = saved
    _, _, pre_last, _, normed_last, rstd_last = last_res
    is_last = section_index == sections - 1
    h_in, agg, act = (jnp.where(is_last, last_res[i], saved[i]) for i in (0, 1, 3))
    saved_out = jnp.where(is_last, last_out, saved_out)

    g = cotangent
    formed = []
    dpre_keep = None
    dout_keep = None
    gain_keep = None
    for tick in range(sections):
        if tick == 0:
            pre_t, normed_t, rstd_t = pre_last, normed_last, rstd_last
        else:
            pre_t, normed_t, rstd_t = pre, normed, rstd
        gf = g.astype(F32)
        gain_term = jnp.sum(gf * normed_t, axis=(0, 1))
        dn = gf * gain_row
        dout = (
            rstd_t
            * (
                dn
                - jnp.mean(dn, axis=-1, keepdims=True)
                - normed_t * jnp.mean(dn * normed_t, axis=-1, keepdims=True)
            )
        ).astype(BF16)
        dact = jnp.einsum("sip,vp->siv", dout, w_2, preferred_element_type=F32)
        sig = jax.nn.sigmoid(pre_t)
        dpre = (dact * sig * (1.0 + pre_t * (1.0 - sig))).astype(BF16)
        gnode = gf + jnp.einsum("sip,vp->siv", dpre, w_a, preferred_element_type=F32)
        dagg = jnp.einsum("sip,vp->siv", dpre, w_b, preferred_element_type=F32).astype(BF16)
        spread = jnp.einsum(
            "ij,sid->sjd", adj2, jnp.concatenate([dagg, dagg], axis=1), preferred_element_type=F32
        )
        left_grad = spread[:, :margin].astype(BF16)
        right_grad = spread[:, margin + nb * blk :].astype(BF16)
        own = gnode + spread[:, margin : margin + nb * blk]

        def finish(partial, from_right, from_left):
            blocks = partial.reshape(samples, nb, blk, width)
            blocks = add_blocks(blocks, send_right, hs, from_right)
            blocks = add_blocks(blocks, send_left, hs, from_left)
            return blocks.reshape(samples, node_rows, width).astype(BF16)

        active = sections - 1 - tick
        mine = section_index == active
        if tick + 1 < sections:
            g = finish(
                lax.ppermute(own.astype(BF16), both, route(active, active - 1, 0)),
                lax.ppermute(left_grad, both, route(active, active - 1, -1)),
                lax.ppermute(right_grad, both, route(active, active - 1, 1)),
            )
            formed.append(g)
            g_new = None
        else:
            g_new = finish(
                own,
                lax.ppermute(left_grad, both, route(active, active, -1)),
                lax.ppermute(right_grad, both, route(active, active, 1)),
            )
        if dpre_keep is None:
            dpre_keep, dout_keep = dpre, dout
            gain_keep = gain_term
        else:
            dpre_keep = jnp.where(mine, dpre, dpre_keep)
            dout_keep = jnp.where(mine, dout, dout_keep)
            gain_keep = jnp.where(mine, gain_term, gain_keep)

    norm_factor = 1.0 / math.sqrt(samples * node_rows * domains)
    stacked = jnp.concatenate([h_in, agg], axis=2)
    gw1 = jnp.einsum("via,vid->ad", stacked, dpre_keep, preferred_element_type=F32)
    gw2 = jnp.einsum("via,vid->ad", act, dout_keep, preferred_element_type=F32)
    r1 = gw1.shape[0] // domains
    r2 = gw2.shape[0] // domains
    r3 = gain_keep.shape[0] // domains
    pad_rows = 16
    gain_rows = jnp.pad(gain_keep.reshape(domains, 1, r3), ((0, 0), (0, pad_rows - 1), (0, width - r3)))
    packed = jnp.concatenate(
        [
            gw1.reshape(domains, r1, width),
            gw2.reshape(domains, r2, width),
            gain_rows,
        ],
        axis=1,
    ).astype(BF16)
    packed = packed.reshape(domains * (r1 + r2 + pad_rows), width)
    reduced = halving_reduce_scatter(packed, "dom", domains, domain_index)
    reduced = reduced.astype(F32) * norm_factor
    g1 = reduced[:r1]
    g2 = reduced[r1 : r1 + r2]
    g3 = reduced[r1 + r2, :r3]
    if formed:
        mine_formed = lax.select_n(
            jnp.clip(sections - 2 - section_index, 0, len(formed) - 1), *formed
        )
        back_pairs = [(linear(d, s), linear(d, s + 1)) for d in range(domains) for s in range(sections - 1)]
        g_back = lax.ppermute(mine_formed, both, back_pairs)
        grad_in = jnp.where(section_index == 0, g_new, g_back)
    else:
        grad_in = g_new
    return (
        saved_out[None],
        grad_in[None],
        g1[None],
        g2[None],
        g3[None],
    )


def solution(mesh):
    return jax.shard_map(
        shards,
        mesh=mesh,
        in_specs=(
            P("groups", "dom", None),
            P("groups", "dom", None),
            P("section", None, None),
            P("section", None, None),
            P("section", None),
            P("dom", None, None),
            P("dom"),
            P("dom"),
            P("dom"),
            P(),
            P(),
        ),
        out_specs=(
            P("section", "groups", "dom", None),
            P("section", "groups", "dom", None),
            P("section", "dom", "groups"),
            P("section", "dom", "groups"),
            P("section", ("groups", "dom")),
        ),
        check_vma=False,
    )
```

```python
import math

import jax
import jax.numpy as jnp
from jax import lax
from jax.sharding import PartitionSpec as P

EPSILON = 1e-05
HIGHEST_PRECISION = lax.Precision.HIGHEST
F32 = jnp.float32
BF16 = jnp.bfloat16


def pick_blocks(blocks, index, count):
    parts = [lax.dynamic_index_in_dim(blocks, index[i], axis=1, keepdims=False) for i in range(count)]
    return jnp.concatenate(parts, axis=1)


def add_blocks(blocks, index, count, values):
    samples, nb, blk, width = blocks.shape
    values = values.reshape(samples, count, blk, width).astype(F32)
    for i in range(count):
        hit = (jnp.arange(nb) == index[i])[None, :, None, None]
        blocks = blocks + jnp.where(hit, values[:, i][:, None], 0.0)
    return blocks


def halving_reduce_scatter(x, axis, devices, index):
    if devices & (devices - 1):
        return lax.psum_scatter(x, axis, scatter_dimension=0, tiled=True)
    rows = x.shape[0] // devices
    cur = x.reshape(devices, rows, x.shape[1]).astype(F32)
    dist = 1
    while dist < devices:
        cur = cur.reshape(cur.shape[0] // 2, 2, rows, x.shape[1])
        bit = (index // dist) % 2
        low, high = cur[:, 0], cur[:, 1]
        keep = jnp.where(bit == 0, low, high)
        send = jnp.where(bit == 0, high, low).astype(x.dtype)
        pairs = [(i, i ^ dist) for i in range(devices)]
        recv = lax.ppermute(send, axis, pairs)
        cur = keep + recv.astype(F32)
        dist *= 2
    return cur[0]


def shards(
    node_input,
    cotangent,
    w_one,
    w_two,
    gain,
    tile_weights,
    tile_rows,
    tile_cols,
    tile_count,
    halo_from_left,
    halo_from_right,
):
    sections = lax.axis_size("section")
    section_index = lax.axis_index("section")
    domains = lax.axis_size("dom")
    domain_index = lax.axis_index("dom")
    samples, node_rows, width = node_input.shape
    slot_count, blk, _ = tile_weights.shape
    nb = node_rows // blk
    hs = halo_from_left.shape[1]
    ext = nb + 2 * hs
    margin = hs * blk
    offset = domain_index * nb
    dom_ids = jnp.arange(domains)[:, None]
    send_right = jnp.sum(jnp.where(dom_ids == (domain_index + 1) % domains, halo_from_left, 0), axis=0) - offset
    send_left = (
        jnp.sum(jnp.where(dom_ids == (domain_index + domains - 1) % domains, halo_from_right, 0), axis=0)
        - offset
    )

    live = (jnp.arange(slot_count) < tile_count[0]).astype(F32)
    row_oh = (tile_rows[:, None] == jnp.arange(nb)[None, :]).astype(F32) * live[:, None]
    col_oh = (tile_cols[:, None] == jnp.arange(ext)[None, :]).astype(F32)
    pair = (row_oh[:, :, None] * col_oh[:, None, :]).reshape(slot_count, nb * ext)
    adj = jnp.einsum("tp,tij->pij", pair, tile_weights.astype(F32), precision=HIGHEST_PRECISION)
    adj = adj.reshape(nb, ext, blk, blk).transpose(0, 2, 1, 3).reshape(nb * blk, ext * blk)
    adj_hi = adj.astype(BF16)
    adj_lo = (adj - adj_hi.astype(F32)).astype(BF16)
    adj2 = jnp.concatenate([adj_hi, adj_lo], axis=0)

    w_a = w_one[0, :width]
    w_b = w_one[0, width:]
    w_2 = w_two[0]
    gain_row = gain[0]

    both = ("dom", "section")

    def linear(d, s):
        return d * sections + s

    def route(src_section, dst_section, shift):
        return [
            (linear(d, src_section), linear((d + shift) % domains, dst_section))
            for d in range(domains)
        ]

    def forward_layer(h, left, right):
        h_ext = jnp.concatenate([left, h, right], axis=1)
        agg2 = jnp.einsum("ij,sjd->sid", adj2, h_ext, preferred_element_type=F32)
        agg = (agg2[:, : nb * blk] + agg2[:, nb * blk :]).astype(BF16)
        pre = jnp.einsum("sic,ct->sit", h, w_a, preferred_element_type=F32)
        pre = pre + jnp.einsum("sic,ct->sit", agg, w_b, preferred_element_type=F32)
        act = jax.nn.silu(pre).astype(BF16)
        mixed = jnp.einsum("sic,ct->sit", act, w_2, preferred_element_type=F32)
        center = mixed - jnp.mean(mixed, axis=-1, keepdims=True)
        rstd = lax.rsqrt(jnp.mean(center * center, axis=-1, keepdims=True) + EPSILON)
        normed = center * rstd
        out = (h.astype(F32) + normed * gain_row).astype(BF16)
        return out, (h, agg, pre, act, normed, rstd)

    in_blocks = node_input.reshape(samples, nb, blk, width)
    left = lax.ppermute(pick_blocks(in_blocks, send_right, hs), both, route(0, 0, 1))
    right = lax.ppermute(pick_blocks(in_blocks, send_left, hs), both, route(0, 0, -1))
    h = node_input
    res_list = []
    out_list = []
    for tick in range(sections):
        out, res = forward_layer(h, left, right)
        res_list.append(res)
        out_list.append(out)
        if tick + 1 < sections:
            out_blocks = out.reshape(samples, nb, blk, width)
            h = lax.ppermute(out, both, route(tick, tick + 1, 0))
            left = lax.ppermute(pick_blocks(out_blocks, send_right, hs), both, route(tick, tick + 1, 1))
            right = lax.ppermute(pick_blocks(out_blocks, send_left, hs), both, route(tick, tick + 1, -1))

    g = cotangent
    formed = []
    dpre_list = []
    dout_list = []
    gain_list = []
    for tick in range(sections):
        _, _, pre_t, _, normed_t, rstd_t = res_list[sections - 1 - tick]
        gf = g.astype(F32)
        gain_term = jnp.sum(gf * normed_t, axis=(0, 1))
        dn = gf * gain_row
        dout = (
            rstd_t
            * (
                dn
                - jnp.mean(dn, axis=-1, keepdims=True)
                - normed_t * jnp.mean(dn * normed_t, axis=-1, keepdims=True)
            )
        ).astype(BF16)
        dact = jnp.einsum("sip,vp->siv", dout, w_2, preferred_element_type=F32)
        sig = jax.nn.sigmoid(pre_t)
        dpre = (dact * sig * (1.0 + pre_t * (1.0 - sig))).astype(BF16)
        gnode = gf + jnp.einsum("sip,vp->siv", dpre, w_a, preferred_element_type=F32)
        dagg = jnp.einsum("sip,vp->siv", dpre, w_b, preferred_element_type=F32).astype(BF16)
        spread = jnp.einsum(
            "ij,sid->sjd", adj2, jnp.concatenate([dagg, dagg], axis=1), preferred_element_type=F32
        )
        left_grad = spread[:, :margin].astype(BF16)
        right_grad = spread[:, margin + nb * blk :].astype(BF16)
        own = gnode + spread[:, margin : margin + nb * blk]

        def finish(partial, from_right, from_left):
            blocks = partial.reshape(samples, nb, blk, width)
            blocks = add_blocks(blocks, send_right, hs, from_right)
            blocks = add_blocks(blocks, send_left, hs, from_left)
            return blocks.reshape(samples, node_rows, width).astype(BF16)

        active = sections - 1 - tick
        mine = section_index == active
        if tick + 1 < sections:
            g = finish(
                lax.ppermute(own.astype(BF16), both, route(active, active - 1, 0)),
                lax.ppermute(left_grad, both, route(active, active - 1, -1)),
                lax.ppermute(right_grad, both, route(active, active - 1, 1)),
            )
            formed.append(g)
            g_new = None
        else:
            g_new = finish(
                own,
                lax.ppermute(left_grad, both, route(active, active, -1)),
                lax.ppermute(right_grad, both, route(active, active, 1)),
            )
        dpre_list.append(dpre)
        dout_list.append(dout)
        gain_list.append(gain_term)

    def own_forward(i):
        return lax.select_n(section_index, *[r[i] for r in res_list])

    def own_backward(values):
        return lax.select_n(sections - 1 - section_index, *values)

    h_in, agg, act = own_forward(0), own_forward(1), own_forward(3)
    saved_out = lax.select_n(section_index, *out_list)
    dpre_keep = own_backward(dpre_list)
    dout_keep = own_backward(dout_list)
    gain_keep = own_backward(gain_list)

    norm_factor = 1.0 / math.sqrt(samples * node_rows * domains)
    stacked = jnp.concatenate([h_in, agg], axis=2)
    gw1 = jnp.einsum("via,vid->ad", stacked, dpre_keep, preferred_element_type=F32)
    gw2 = jnp.einsum("via,vid->ad", act, dout_keep, preferred_element_type=F32)
    r1 = gw1.shape[0] // domains
    r2 = gw2.shape[0] // domains
    r3 = gain_keep.shape[0] // domains
    pad_rows = 16
    gain_rows = jnp.pad(gain_keep.reshape(domains, 1, r3), ((0, 0), (0, pad_rows - 1), (0, width - r3)))
    packed = jnp.concatenate(
        [
            gw1.reshape(domains, r1, width),
            gw2.reshape(domains, r2, width),
            gain_rows,
        ],
        axis=1,
    ).astype(BF16)
    packed = packed.reshape(domains * (r1 + r2 + pad_rows), width)
    reduced = halving_reduce_scatter(packed, "dom", domains, domain_index)
    reduced = reduced.astype(F32) * norm_factor
    g1 = reduced[:r1]
    g2 = reduced[r1 : r1 + r2]
    g3 = reduced[r1 + r2, :r3]
    if formed:
        mine_formed = lax.select_n(
            jnp.clip(sections - 2 - section_index, 0, len(formed) - 1), *formed
        )
        back_pairs = [(linear(d, s), linear(d, s + 1)) for d in range(domains) for s in range(sections - 1)]
        g_back = lax.ppermute(mine_formed, both, back_pairs)
        grad_in = jnp.where(section_index == 0, g_new, g_back)
    else:
        grad_in = g_new
    return (
        saved_out[None],
        grad_in[None],
        g1[None],
        g2[None],
        g3[None],
    )


def solution(mesh):
    return jax.shard_map(
        shards,
        mesh=mesh,
        in_specs=(
            P("groups", "dom", None),
            P("groups", "dom", None),
            P("section", None, None),
            P("section", None, None),
            P("section", None),
            P("dom", None, None),
            P("dom"),
            P("dom"),
            P("dom"),
            P(),
            P(),
        ),
        out_specs=(
            P("section", "groups", "dom", None),
            P("section", "groups", "dom", None),
            P("section", "dom", "groups"),
            P("section", "dom", "groups"),
            P("section", ("groups", "dom")),
        ),
        check_vma=False,
    )
```

```python
import math

import jax
import jax.numpy as jnp
from jax import lax
from jax.sharding import PartitionSpec as P

EPSILON = 1e-05
HIGHEST_PRECISION = lax.Precision.HIGHEST
F32 = jnp.float32
BF16 = jnp.bfloat16


def pick_blocks(blocks, index, count):
    parts = [lax.dynamic_index_in_dim(blocks, index[i], axis=1, keepdims=False) for i in range(count)]
    return jnp.concatenate(parts, axis=1)


def add_blocks(blocks, index, count, values):
    samples, nb, blk, width = blocks.shape
    values = values.reshape(samples, count, blk, width).astype(F32)
    for i in range(count):
        hit = (jnp.arange(nb) == index[i])[None, :, None, None]
        blocks = blocks + jnp.where(hit, values[:, i][:, None], 0.0)
    return blocks


def halving_reduce_scatter(x, axis, devices, index):
    if devices & (devices - 1):
        return lax.psum_scatter(x, axis, scatter_dimension=0, tiled=True)
    rows = x.shape[0] // devices
    cur = x.reshape(devices, rows, x.shape[1]).astype(F32)
    dist = 1
    while dist < devices:
        cur = cur.reshape(cur.shape[0] // 2, 2, rows, x.shape[1])
        bit = (index // dist) % 2
        low, high = cur[:, 0], cur[:, 1]
        keep = jnp.where(bit == 0, low, high)
        send = jnp.where(bit == 0, high, low).astype(x.dtype)
        pairs = [(i, i ^ dist) for i in range(devices)]
        recv = lax.ppermute(send, axis, pairs)
        cur = keep + recv.astype(F32)
        dist *= 2
    return cur[0]


def shards(
    node_input,
    cotangent,
    w_one,
    w_two,
    gain,
    tile_weights,
    tile_rows,
    tile_cols,
    tile_count,
    halo_from_left,
    halo_from_right,
):
    sections = lax.axis_size("section")
    section_index = lax.axis_index("section")
    domains = lax.axis_size("dom")
    domain_index = lax.axis_index("dom")
    samples, node_rows, width = node_input.shape
    slot_count, blk, _ = tile_weights.shape
    nb = node_rows // blk
    hs = halo_from_left.shape[1]
    ext = nb + 2 * hs
    margin = hs * blk
    offset = domain_index * nb
    dom_ids = jnp.arange(domains)[:, None]
    send_right = jnp.sum(jnp.where(dom_ids == (domain_index + 1) % domains, halo_from_left, 0), axis=0) - offset
    send_left = (
        jnp.sum(jnp.where(dom_ids == (domain_index + domains - 1) % domains, halo_from_right, 0), axis=0)
        - offset
    )

    live = (jnp.arange(slot_count) < tile_count[0]).astype(F32)
    row_oh = (tile_rows[:, None] == jnp.arange(nb)[None, :]).astype(F32) * live[:, None]
    col_oh = (tile_cols[:, None] == jnp.arange(ext)[None, :]).astype(F32)
    pair = (row_oh[:, :, None] * col_oh[:, None, :]).reshape(slot_count, nb * ext)
    adj = jnp.einsum("tp,tij->pij", pair, tile_weights.astype(F32), precision=HIGHEST_PRECISION)
    adj = adj.reshape(nb, ext, blk, blk).transpose(0, 2, 1, 3).reshape(nb * blk, ext * blk)
    adj_hi = adj.astype(BF16)
    adj_lo = (adj - adj_hi.astype(F32)).astype(BF16)
    adj2 = jnp.concatenate([adj_hi, adj_lo], axis=0)

    w_a = w_one[0, :width]
    w_b = w_one[0, width:]
    w_2 = w_two[0]
    gain_row = gain[0]

    both = ("dom", "section")

    def linear(d, s):
        return d * sections + s

    def route(src_section, dst_section, shift):
        return [
            (linear(d, src_section), linear((d + shift) % domains, dst_section))
            for d in range(domains)
        ]

    def forward_layer(h, left, right):
        h_ext = jnp.concatenate([left, h, right], axis=1)
        agg2 = jnp.einsum("ij,sjd->sid", adj2, h_ext, preferred_element_type=F32)
        agg = (agg2[:, : nb * blk] + agg2[:, nb * blk :]).astype(BF16)
        pre = jnp.einsum("sic,ct->sit", h, w_a, preferred_element_type=F32)
        pre = pre + jnp.einsum("sic,ct->sit", agg, w_b, preferred_element_type=F32)
        act = jax.nn.silu(pre).astype(BF16)
        mixed = jnp.einsum("sic,ct->sit", act, w_2, preferred_element_type=F32)
        center = mixed - jnp.mean(mixed, axis=-1, keepdims=True)
        rstd = lax.rsqrt(jnp.mean(center * center, axis=-1, keepdims=True) + EPSILON)
        normed = center * rstd
        out = (h.astype(F32) + normed * gain_row).astype(BF16)
        return out, (h, agg, pre, act, normed, rstd)

    in_blocks = node_input.reshape(samples, nb, blk, width)
    left = lax.ppermute(pick_blocks(in_blocks, send_right, hs), both, route(0, 0, 1))
    right = lax.ppermute(pick_blocks(in_blocks, send_left, hs), both, route(0, 0, -1))
    h = node_input
    res_list = []
    out_list = []
    for tick in range(sections):
        out, res = forward_layer(h, left, right)
        res_list.append(res)
        out_list.append(out)
        if tick + 1 < sections:
            out_blocks = out.reshape(samples, nb, blk, width)
            h = lax.ppermute(out, both, route(tick, tick + 1, 0))
            left = lax.ppermute(pick_blocks(out_blocks, send_right, hs), both, route(tick, tick + 1, 1))
            right = lax.ppermute(pick_blocks(out_blocks, send_left, hs), both, route(tick, tick + 1, -1))

    g = cotangent
    formed = []
    dpre_list = []
    dout_list = []
    gain_list = []
    for tick in range(sections):
        _, _, pre_t, _, normed_t, rstd_t = res_list[sections - 1 - tick]
        gf = g.astype(F32)
        gain_term = jnp.sum(gf * normed_t, axis=(0, 1))
        dn = gf * gain_row
        dout = (
            rstd_t
            * (
                dn
                - jnp.mean(dn, axis=-1, keepdims=True)
                - normed_t * jnp.mean(dn * normed_t, axis=-1, keepdims=True)
            )
        ).astype(BF16)
        dact = jnp.einsum("sip,vp->siv", dout, w_2, preferred_element_type=F32)
        sig = jax.nn.sigmoid(pre_t)
        dpre = (dact * sig * (1.0 + pre_t * (1.0 - sig))).astype(BF16)
        gnode = gf + jnp.einsum("sip,vp->siv", dpre, w_a, preferred_element_type=F32)
        dagg = jnp.einsum("sip,vp->siv", dpre, w_b, preferred_element_type=F32).astype(BF16)
        spread = jnp.einsum(
            "ij,sid->sjd", adj2, jnp.concatenate([dagg, dagg], axis=1), preferred_element_type=F32
        )
        left_grad = spread[:, :margin].astype(BF16)
        right_grad = spread[:, margin + nb * blk :].astype(BF16)
        own = gnode + spread[:, margin : margin + nb * blk]

        def finish(partial, from_right, from_left):
            blocks = partial.reshape(samples, nb, blk, width)
            blocks = add_blocks(blocks, send_right, hs, from_right)
            blocks = add_blocks(blocks, send_left, hs, from_left)
            return blocks.reshape(samples, node_rows, width).astype(BF16)

        active = sections - 1 - tick
        mine = section_index == active
        if tick + 1 < sections:
            g = finish(
                lax.ppermute(own.astype(BF16), both, route(active, active - 1, 0)),
                lax.ppermute(left_grad, both, route(active, active - 1, -1)),
                lax.ppermute(right_grad, both, route(active, active - 1, 1)),
            )
            formed.append(g)
            g_new = None
        else:
            g_new = finish(
                own,
                lax.ppermute(left_grad, both, route(active, active, -1)),
                lax.ppermute(right_grad, both, route(active, active, 1)),
            )
        dpre_list.append(dpre)
        dout_list.append(dout)
        gain_list.append(gain_term)

    late_index, _ = lax.optimization_barrier((section_index, dpre))

    def own_forward(i):
        return lax.select_n(late_index, *[r[i] for r in res_list])

    def own_backward(values):
        return lax.select_n(sections - 1 - section_index, *values)

    h_in, agg, act = own_forward(0), own_forward(1), own_forward(3)
    saved_out = lax.select_n(late_index, *out_list)
    dpre_keep = own_backward(dpre_list)
    dout_keep = own_backward(dout_list)
    gain_keep = own_backward(gain_list)

    norm_factor = 1.0 / math.sqrt(samples * node_rows * domains)
    stacked = jnp.concatenate([h_in, agg], axis=2)
    gw1 = jnp.einsum("via,vid->ad", stacked, dpre_keep, preferred_element_type=F32)
    gw2 = jnp.einsum("via,vid->ad", act, dout_keep, preferred_element_type=F32)
    r1 = gw1.shape[0] // domains
    r2 = gw2.shape[0] // domains
    r3 = gain_keep.shape[0] // domains
    pad_rows = 16
    gain_rows = jnp.pad(gain_keep.reshape(domains, 1, r3), ((0, 0), (0, pad_rows - 1), (0, width - r3)))
    packed = jnp.concatenate(
        [
            gw1.reshape(domains, r1, width),
            gw2.reshape(domains, r2, width),
            gain_rows,
        ],
        axis=1,
    ).astype(BF16)
    packed = packed.reshape(domains * (r1 + r2 + pad_rows), width)
    reduced = halving_reduce_scatter(packed, "dom", domains, domain_index)
    reduced = reduced.astype(F32) * norm_factor
    g1 = reduced[:r1]
    g2 = reduced[r1 : r1 + r2]
    g3 = reduced[r1 + r2, :r3]
    if formed:
        mine_formed = lax.select_n(
            jnp.clip(sections - 2 - late_index, 0, len(formed) - 1), *formed
        )
        back_pairs = [(linear(d, s), linear(d, s + 1)) for d in range(domains) for s in range(sections - 1)]
        g_back = lax.ppermute(mine_formed, both, back_pairs)
        grad_in = jnp.where(section_index == 0, g_new, g_back)
    else:
        grad_in = g_new
    return (
        saved_out[None],
        grad_in[None],
        g1[None],
        g2[None],
        g3[None],
    )


def solution(mesh):
    return jax.shard_map(
        shards,
        mesh=mesh,
        in_specs=(
            P("groups", "dom", None),
            P("groups", "dom", None),
            P("section", None, None),
            P("section", None, None),
            P("section", None),
            P("dom", None, None),
            P("dom"),
            P("dom"),
            P("dom"),
            P(),
            P(),
        ),
        out_specs=(
            P("section", "groups", "dom", None),
            P("section", "groups", "dom", None),
            P("section", "dom", "groups"),
            P("section", "dom", "groups"),
            P("section", ("groups", "dom")),
        ),
        check_vma=False,
    )
```

```python
import math

import jax
import jax.numpy as jnp
from jax import lax
from jax.sharding import PartitionSpec as P

EPSILON = 1e-05
HIGHEST_PRECISION = lax.Precision.HIGHEST
F32 = jnp.float32
BF16 = jnp.bfloat16


def pick_blocks(blocks, index, count):
    parts = [lax.dynamic_index_in_dim(blocks, index[i], axis=1, keepdims=False) for i in range(count)]
    return jnp.concatenate(parts, axis=1)


def add_blocks(blocks, index, count, values):
    samples, nb, blk, width = blocks.shape
    values = values.reshape(samples, count, blk, width).astype(F32)
    for i in range(count):
        hit = (jnp.arange(nb) == index[i])[None, :, None, None]
        blocks = blocks + jnp.where(hit, values[:, i][:, None], 0.0)
    return blocks


def halving_reduce_scatter(x, axis, devices, index):
    if devices & (devices - 1):
        return lax.psum_scatter(x, axis, scatter_dimension=0, tiled=True)
    rows = x.shape[0] // devices
    cur = x.reshape(devices, rows, x.shape[1]).astype(F32)
    dist = 1
    while dist < devices:
        cur = cur.reshape(cur.shape[0] // 2, 2, rows, x.shape[1])
        bit = (index // dist) % 2
        low, high = cur[:, 0], cur[:, 1]
        keep = jnp.where(bit == 0, low, high)
        send = jnp.where(bit == 0, high, low).astype(x.dtype)
        pairs = [(i, i ^ dist) for i in range(devices)]
        recv = lax.ppermute(send, axis, pairs)
        cur = keep + recv.astype(F32)
        dist *= 2
    return cur[0]


def shards(
    node_input,
    cotangent,
    w_one,
    w_two,
    gain,
    tile_weights,
    tile_rows,
    tile_cols,
    tile_count,
    halo_from_left,
    halo_from_right,
):
    sections = lax.axis_size("section")
    section_index = lax.axis_index("section")
    domains = lax.axis_size("dom")
    domain_index = lax.axis_index("dom")
    samples, node_rows, width = node_input.shape
    slot_count, blk, _ = tile_weights.shape
    nb = node_rows // blk
    hs = halo_from_left.shape[1]
    ext = nb + 2 * hs
    margin = hs * blk
    offset = domain_index * nb
    dom_ids = jnp.arange(domains)[:, None]
    send_right = jnp.sum(jnp.where(dom_ids == (domain_index + 1) % domains, halo_from_left, 0), axis=0) - offset
    send_left = (
        jnp.sum(jnp.where(dom_ids == (domain_index + domains - 1) % domains, halo_from_right, 0), axis=0)
        - offset
    )

    live = (jnp.arange(slot_count) < tile_count[0]).astype(F32)
    row_oh = (tile_rows[:, None] == jnp.arange(nb)[None, :]).astype(F32) * live[:, None]
    col_oh = (tile_cols[:, None] == jnp.arange(ext)[None, :]).astype(F32)
    pair = (row_oh[:, :, None] * col_oh[:, None, :]).reshape(slot_count, nb * ext)
    adj = jnp.einsum("tp,tij->pij", pair, tile_weights.astype(F32), precision=HIGHEST_PRECISION)
    adj = adj.reshape(nb, ext, blk, blk).transpose(0, 2, 1, 3).reshape(nb * blk, ext * blk)
    adj_hi = adj.astype(BF16)
    adj_lo = (adj - adj_hi.astype(F32)).astype(BF16)
    adj2 = jnp.concatenate([adj_hi, adj_lo], axis=0)

    w_full = w_one[0]
    w_2 = w_two[0]
    gain_row = gain[0]

    both = ("dom", "section")

    def linear(d, s):
        return d * sections + s

    def route(src_section, dst_section, shift):
        return [
            (linear(d, src_section), linear((d + shift) % domains, dst_section))
            for d in range(domains)
        ]

    def forward_layer(h, left, right):
        h_ext = jnp.concatenate([left, h, right], axis=1)
        agg2 = jnp.einsum("ij,sjd->sid", adj2, h_ext, preferred_element_type=F32)
        agg = (agg2[:, : nb * blk] + agg2[:, nb * blk :]).astype(BF16)
        pre = jnp.einsum("sic,ct->sit", h, w_full[:width], preferred_element_type=F32)
        pre = pre + jnp.einsum("sic,ct->sit", agg, w_full[width:], preferred_element_type=F32)
        act = jax.nn.silu(pre).astype(BF16)
        mixed = jnp.einsum("sic,ct->sit", act, w_2, preferred_element_type=F32)
        center = mixed - jnp.mean(mixed, axis=-1, keepdims=True)
        rstd = lax.rsqrt(jnp.mean(center * center, axis=-1, keepdims=True) + EPSILON)
        normed = center * rstd
        out = (h.astype(F32) + normed * gain_row).astype(BF16)
        return out, (h, agg, pre, act, normed, rstd)

    in_blocks = node_input.reshape(samples, nb, blk, width)
    left = lax.ppermute(pick_blocks(in_blocks, send_right, hs), both, route(0, 0, 1))
    right = lax.ppermute(pick_blocks(in_blocks, send_left, hs), both, route(0, 0, -1))
    h = node_input
    res_list = []
    out_list = []
    for tick in range(sections):
        out, res = forward_layer(h, left, right)
        res_list.append(res)
        out_list.append(out)
        if tick + 1 < sections:
            out_blocks = out.reshape(samples, nb, blk, width)
            h = lax.ppermute(out, both, route(tick, tick + 1, 0))
            left = lax.ppermute(pick_blocks(out_blocks, send_right, hs), both, route(tick, tick + 1, 1))
            right = lax.ppermute(pick_blocks(out_blocks, send_left, hs), both, route(tick, tick + 1, -1))

    g = cotangent
    formed = []
    dpre_list = []
    dout_list = []
    gain_list = []
    for tick in range(sections):
        _, _, pre_t, _, normed_t, rstd_t = res_list[sections - 1 - tick]
        gf = g.astype(F32)
        gain_term = jnp.sum(gf * normed_t, axis=(0, 1))
        dn = gf * gain_row
        dout = (
            rstd_t
            * (
                dn
                - jnp.mean(dn, axis=-1, keepdims=True)
                - normed_t * jnp.mean(dn * normed_t, axis=-1, keepdims=True)
            )
        ).astype(BF16)
        dact = jnp.einsum("sip,vp->siv", dout, w_2, preferred_element_type=F32)
        sig = jax.nn.sigmoid(pre_t)
        dpre = (dact * sig * (1.0 + pre_t * (1.0 - sig))).astype(BF16)
        both_grads = jnp.einsum("sip,vp->siv", dpre, w_full, preferred_element_type=F32)
        gnode = gf + both_grads[:, :, :width]
        dagg = both_grads[:, :, width:].astype(BF16)
        spread = jnp.einsum(
            "ij,sid->sjd", adj2, jnp.concatenate([dagg, dagg], axis=1), preferred_element_type=F32
        )
        left_grad = spread[:, :margin].astype(BF16)
        right_grad = spread[:, margin + nb * blk :].astype(BF16)
        own = gnode + spread[:, margin : margin + nb * blk]

        def finish(partial, from_right, from_left):
            blocks = partial.reshape(samples, nb, blk, width)
            blocks = add_blocks(blocks, send_right, hs, from_right)
            blocks = add_blocks(blocks, send_left, hs, from_left)
            return blocks.reshape(samples, node_rows, width).astype(BF16)

        active = sections - 1 - tick
        mine = section_index == active
        if tick + 1 < sections:
            g = finish(
                lax.ppermute(own.astype(BF16), both, route(active, active - 1, 0)),
                lax.ppermute(left_grad, both, route(active, active - 1, -1)),
                lax.ppermute(right_grad, both, route(active, active - 1, 1)),
            )
            formed.append(g)
            g_new = None
        else:
            g_new = finish(
                own,
                lax.ppermute(left_grad, both, route(active, active, -1)),
                lax.ppermute(right_grad, both, route(active, active, 1)),
            )
        dpre_list.append(dpre)
        dout_list.append(dout)
        gain_list.append(gain_term)

    def own_forward(i):
        return lax.select_n(section_index, *[r[i] for r in res_list])

    def own_backward(values):
        return lax.select_n(sections - 1 - section_index, *values)

    h_in, agg, act = own_forward(0), own_forward(1), own_forward(3)
    saved_out = lax.select_n(section_index, *out_list)
    dpre_keep = own_backward(dpre_list)
    dout_keep = own_backward(dout_list)
    gain_keep = own_backward(gain_list)

    norm_factor = 1.0 / math.sqrt(samples * node_rows * domains)
    stacked = jnp.concatenate([h_in, agg], axis=2)
    gw1 = jnp.einsum("via,vid->ad", stacked, dpre_keep, preferred_element_type=F32)
    gw2 = jnp.einsum("via,vid->ad", act, dout_keep, preferred_element_type=F32)
    r1 = gw1.shape[0] // domains
    r2 = gw2.shape[0] // domains
    r3 = gain_keep.shape[0] // domains
    pad_rows = 16
    gain_rows = jnp.pad(gain_keep.reshape(domains, 1, r3), ((0, 0), (0, pad_rows - 1), (0, width - r3)))
    packed = jnp.concatenate(
        [
            gw1.reshape(domains, r1, width),
            gw2.reshape(domains, r2, width),
            gain_rows,
        ],
        axis=1,
    ).astype(BF16)
    packed = packed.reshape(domains * (r1 + r2 + pad_rows), width)
    reduced = halving_reduce_scatter(packed, "dom", domains, domain_index)
    reduced = reduced.astype(F32) * norm_factor
    g1 = reduced[:r1]
    g2 = reduced[r1 : r1 + r2]
    g3 = reduced[r1 + r2, :r3]
    if formed:
        mine_formed = lax.select_n(
            jnp.clip(sections - 2 - section_index, 0, len(formed) - 1), *formed
        )
        back_pairs = [(linear(d, s), linear(d, s + 1)) for d in range(domains) for s in range(sections - 1)]
        g_back = lax.ppermute(mine_formed, both, back_pairs)
        grad_in = jnp.where(section_index == 0, g_new, g_back)
    else:
        grad_in = g_new
    return (
        saved_out[None],
        grad_in[None],
        g1[None],
        g2[None],
        g3[None],
    )


def solution(mesh):
    return jax.shard_map(
        shards,
        mesh=mesh,
        in_specs=(
            P("groups", "dom", None),
            P("groups", "dom", None),
            P("section", None, None),
            P("section", None, None),
            P("section", None),
            P("dom", None, None),
            P("dom"),
            P("dom"),
            P("dom"),
            P(),
            P(),
        ),
        out_specs=(
            P("section", "groups", "dom", None),
            P("section", "groups", "dom", None),
            P("section", "dom", "groups"),
            P("section", "dom", "groups"),
            P("section", ("groups", "dom")),
        ),
        check_vma=False,
    )
```

```python
import math

import jax
import jax.numpy as jnp
from jax import lax
from jax.sharding import PartitionSpec as P

EPSILON = 1e-05
HIGHEST_PRECISION = lax.Precision.HIGHEST
F32 = jnp.float32
BF16 = jnp.bfloat16


def pick_blocks(blocks, index, count):
    parts = [lax.dynamic_index_in_dim(blocks, index[i], axis=1, keepdims=False) for i in range(count)]
    return jnp.concatenate(parts, axis=1)


def add_blocks(blocks, index, count, values):
    samples, nb, blk, width = blocks.shape
    values = values.reshape(samples, count, blk, width).astype(F32)
    for i in range(count):
        hit = (jnp.arange(nb) == index[i])[None, :, None, None]
        blocks = blocks + jnp.where(hit, values[:, i][:, None], 0.0)
    return blocks


def halving_reduce_scatter(x, axis, devices, index):
    if devices & (devices - 1):
        return lax.psum_scatter(x, axis, scatter_dimension=0, tiled=True)
    rows = x.shape[0] // devices
    cur = x.reshape(devices, rows, x.shape[1]).astype(F32)
    dist = 1
    while dist < devices:
        cur = cur.reshape(cur.shape[0] // 2, 2, rows, x.shape[1])
        bit = (index // dist) % 2
        low, high = cur[:, 0], cur[:, 1]
        keep = jnp.where(bit == 0, low, high)
        send = jnp.where(bit == 0, high, low).astype(x.dtype)
        pairs = [(i, i ^ dist) for i in range(devices)]
        recv = lax.ppermute(send, axis, pairs)
        cur = keep + recv.astype(F32)
        dist *= 2
    return cur[0]


def shards(
    node_input,
    cotangent,
    w_one,
    w_two,
    gain,
    tile_weights,
    tile_rows,
    tile_cols,
    tile_count,
    halo_from_left,
    halo_from_right,
):
    sections = lax.axis_size("section")
    section_index = lax.axis_index("section")
    domains = lax.axis_size("dom")
    domain_index = lax.axis_index("dom")
    samples, node_rows, width = node_input.shape
    slot_count, blk, _ = tile_weights.shape
    nb = node_rows // blk
    hs = halo_from_left.shape[1]
    ext = nb + 2 * hs
    margin = hs * blk
    offset = domain_index * nb
    dom_ids = jnp.arange(domains)[:, None]
    send_right = jnp.sum(jnp.where(dom_ids == (domain_index + 1) % domains, halo_from_left, 0), axis=0) - offset
    send_left = (
        jnp.sum(jnp.where(dom_ids == (domain_index + domains - 1) % domains, halo_from_right, 0), axis=0)
        - offset
    )

    live = (jnp.arange(slot_count) < tile_count[0]).astype(F32)
    row_oh = (tile_rows[:, None] == jnp.arange(nb)[None, :]).astype(F32) * live[:, None]
    col_oh = (tile_cols[:, None] == jnp.arange(ext)[None, :]).astype(F32)
    pair = (row_oh[:, :, None] * col_oh[:, None, :]).reshape(slot_count, nb * ext)
    adj = jnp.einsum("tp,tij->pij", pair, tile_weights.astype(F32), precision=HIGHEST_PRECISION)
    adj = adj.reshape(nb, ext, blk, blk).transpose(0, 2, 1, 3).reshape(nb * blk, ext * blk)
    adj_hi = adj.astype(BF16)
    adj_lo = (adj - adj_hi.astype(F32)).astype(BF16)
    adj2 = jnp.concatenate([adj_hi, adj_lo], axis=0)

    w_a = w_one[0, :width]
    w_b = w_one[0, width:]
    w_2 = w_two[0]
    gain_row = gain[0]

    both = ("dom", "section")

    def linear(d, s):
        return d * sections + s

    def route(src_section, dst_section, shift):
        return [
            (linear(d, src_section), linear((d + shift) % domains, dst_section))
            for d in range(domains)
        ]

    def forward_layer(h, left, right, split=False):
        if split:
            agg2 = jnp.einsum(
                "ij,sjd->sid", adj2[:, margin : margin + nb * blk], h, preferred_element_type=F32
            )
            halo = jnp.concatenate([left, right], axis=1)
            adj_halo = jnp.concatenate([adj2[:, :margin], adj2[:, margin + nb * blk :]], axis=1)
            agg2 = agg2 + jnp.einsum("ij,sjd->sid", adj_halo, halo, preferred_element_type=F32)
        else:
            h_ext = jnp.concatenate([left, h, right], axis=1)
            agg2 = jnp.einsum("ij,sjd->sid", adj2, h_ext, preferred_element_type=F32)
        agg = (agg2[:, : nb * blk] + agg2[:, nb * blk :]).astype(BF16)
        pre = jnp.einsum("sic,ct->sit", h, w_a, preferred_element_type=F32)
        pre = pre + jnp.einsum("sic,ct->sit", agg, w_b, preferred_element_type=F32)
        act = jax.nn.silu(pre).astype(BF16)
        mixed = jnp.einsum("sic,ct->sit", act, w_2, preferred_element_type=F32)
        center = mixed - jnp.mean(mixed, axis=-1, keepdims=True)
        rstd = lax.rsqrt(jnp.mean(center * center, axis=-1, keepdims=True) + EPSILON)
        normed = center * rstd
        out = (h.astype(F32) + normed * gain_row).astype(BF16)
        return out, (h, agg, pre, act, normed, rstd)

    in_blocks = node_input.reshape(samples, nb, blk, width)
    left = lax.ppermute(pick_blocks(in_blocks, send_right, hs), both, route(0, 0, 1))
    right = lax.ppermute(pick_blocks(in_blocks, send_left, hs), both, route(0, 0, -1))
    h = node_input
    res_list = []
    out_list = []
    for tick in range(sections):
        out, res = forward_layer(h, left, right, split=tick == 0)
        res_list.append(res)
        out_list.append(out)
        if tick + 1 < sections:
            out_blocks = out.reshape(samples, nb, blk, width)
            h = lax.ppermute(out, both, route(tick, tick + 1, 0))
            left = lax.ppermute(pick_blocks(out_blocks, send_right, hs), both, route(tick, tick + 1, 1))
            right = lax.ppermute(pick_blocks(out_blocks, send_left, hs), both, route(tick, tick + 1, -1))

    g = cotangent
    formed = []
    dpre_list = []
    dout_list = []
    gain_list = []
    for tick in range(sections):
        _, _, pre_t, _, normed_t, rstd_t = res_list[sections - 1 - tick]
        gf = g.astype(F32)
        gain_term = jnp.sum(gf * normed_t, axis=(0, 1))
        dn = gf * gain_row
        dout = (
            rstd_t
            * (
                dn
                - jnp.mean(dn, axis=-1, keepdims=True)
                - normed_t * jnp.mean(dn * normed_t, axis=-1, keepdims=True)
            )
        ).astype(BF16)
        dact = jnp.einsum("sip,vp->siv", dout, w_2, preferred_element_type=F32)
        sig = jax.nn.sigmoid(pre_t)
        dpre = (dact * sig * (1.0 + pre_t * (1.0 - sig))).astype(BF16)
        gnode = gf + jnp.einsum("sip,vp->siv", dpre, w_a, preferred_element_type=F32)
        dagg = jnp.einsum("sip,vp->siv", dpre, w_b, preferred_element_type=F32).astype(BF16)
        spread = jnp.einsum(
            "ij,sid->sjd", adj2, jnp.concatenate([dagg, dagg], axis=1), preferred_element_type=F32
        )
        left_grad = spread[:, :margin].astype(BF16)
        right_grad = spread[:, margin + nb * blk :].astype(BF16)
        own = gnode + spread[:, margin : margin + nb * blk]

        def finish(partial, from_right, from_left):
            blocks = partial.reshape(samples, nb, blk, width)
            blocks = add_blocks(blocks, send_right, hs, from_right)
            blocks = add_blocks(blocks, send_left, hs, from_left)
            return blocks.reshape(samples, node_rows, width).astype(BF16)

        active = sections - 1 - tick
        mine = section_index == active
        if tick + 1 < sections:
            g = finish(
                lax.ppermute(own.astype(BF16), both, route(active, active - 1, 0)),
                lax.ppermute(left_grad, both, route(active, active - 1, -1)),
                lax.ppermute(right_grad, both, route(active, active - 1, 1)),
            )
            formed.append(g)
            g_new = None
        else:
            g_new = finish(
                own,
                lax.ppermute(left_grad, both, route(active, active, -1)),
                lax.ppermute(right_grad, both, route(active, active, 1)),
            )
        dpre_list.append(dpre)
        dout_list.append(dout)
        gain_list.append(gain_term)

    def own_forward(i):
        return lax.select_n(section_index, *[r[i] for r in res_list])

    def own_backward(values):
        return lax.select_n(sections - 1 - section_index, *values)

    h_in, agg, act = own_forward(0), own_forward(1), own_forward(3)
    saved_out = lax.select_n(section_index, *out_list)
    dpre_keep = own_backward(dpre_list)
    dout_keep = own_backward(dout_list)
    gain_keep = own_backward(gain_list)

    norm_factor = 1.0 / math.sqrt(samples * node_rows * domains)
    stacked = jnp.concatenate([h_in, agg], axis=2)
    gw1 = jnp.einsum("via,vid->ad", stacked, dpre_keep, preferred_element_type=F32)
    gw2 = jnp.einsum("via,vid->ad", act, dout_keep, preferred_element_type=F32)
    r1 = gw1.shape[0] // domains
    r2 = gw2.shape[0] // domains
    r3 = gain_keep.shape[0] // domains
    pad_rows = 16
    gain_rows = jnp.pad(gain_keep.reshape(domains, 1, r3), ((0, 0), (0, pad_rows - 1), (0, width - r3)))
    packed = jnp.concatenate(
        [
            gw1.reshape(domains, r1, width),
            gw2.reshape(domains, r2, width),
            gain_rows,
        ],
        axis=1,
    ).astype(BF16)
    packed = packed.reshape(domains * (r1 + r2 + pad_rows), width)
    reduced = halving_reduce_scatter(packed, "dom", domains, domain_index)
    reduced = reduced.astype(F32) * norm_factor
    g1 = reduced[:r1]
    g2 = reduced[r1 : r1 + r2]
    g3 = reduced[r1 + r2, :r3]
    if formed:
        mine_formed = lax.select_n(
            jnp.clip(sections - 2 - section_index, 0, len(formed) - 1), *formed
        )
        back_pairs = [(linear(d, s), linear(d, s + 1)) for d in range(domains) for s in range(sections - 1)]
        g_back = lax.ppermute(mine_formed, both, back_pairs)
        grad_in = jnp.where(section_index == 0, g_new, g_back)
    else:
        grad_in = g_new
    return (
        saved_out[None],
        grad_in[None],
        g1[None],
        g2[None],
        g3[None],
    )


def solution(mesh):
    return jax.shard_map(
        shards,
        mesh=mesh,
        in_specs=(
            P("groups", "dom", None),
            P("groups", "dom", None),
            P("section", None, None),
            P("section", None, None),
            P("section", None),
            P("dom", None, None),
            P("dom"),
            P("dom"),
            P("dom"),
            P(),
            P(),
        ),
        out_specs=(
            P("section", "groups", "dom", None),
            P("section", "groups", "dom", None),
            P("section", "dom", "groups"),
            P("section", "dom", "groups"),
            P("section", ("groups", "dom")),
        ),
        check_vma=False,
    )
```

```python
import math

import jax
import jax.numpy as jnp
from jax import lax
from jax.sharding import PartitionSpec as P

EPSILON = 1e-05
HIGHEST_PRECISION = lax.Precision.HIGHEST
F32 = jnp.float32
BF16 = jnp.bfloat16


def pick_blocks(blocks, index, count):
    parts = [lax.dynamic_index_in_dim(blocks, index[i], axis=1, keepdims=False) for i in range(count)]
    return jnp.concatenate(parts, axis=1)


def add_blocks(blocks, index, count, values):
    samples, nb, blk, width = blocks.shape
    values = values.reshape(samples, count, blk, width).astype(F32)
    for i in range(count):
        hit = (jnp.arange(nb) == index[i])[None, :, None, None]
        blocks = blocks + jnp.where(hit, values[:, i][:, None], 0.0)
    return blocks


def halving_reduce_scatter(x, axis, devices, index):
    if devices & (devices - 1):
        return lax.psum_scatter(x, axis, scatter_dimension=0, tiled=True)
    rows = x.shape[0] // devices
    cur = x.reshape(devices, rows, x.shape[1]).astype(F32)
    dist = 1
    while dist < devices:
        cur = cur.reshape(cur.shape[0] // 2, 2, rows, x.shape[1])
        bit = (index // dist) % 2
        low, high = cur[:, 0], cur[:, 1]
        keep = jnp.where(bit == 0, low, high)
        send = jnp.where(bit == 0, high, low).astype(x.dtype)
        pairs = [(i, i ^ dist) for i in range(devices)]
        recv = lax.ppermute(send, axis, pairs)
        cur = keep + recv.astype(F32)
        dist *= 2
    return cur[0]


def shards(
    node_input,
    cotangent,
    w_one,
    w_two,
    gain,
    tile_weights,
    tile_rows,
    tile_cols,
    tile_count,
    halo_from_left,
    halo_from_right,
):
    sections = lax.axis_size("section")
    section_index = lax.axis_index("section")
    domains = lax.axis_size("dom")
    domain_index = lax.axis_index("dom")
    samples, node_rows, width = node_input.shape
    slot_count, blk, _ = tile_weights.shape
    nb = node_rows // blk
    hs = halo_from_left.shape[1]
    ext = nb + 2 * hs
    margin = hs * blk
    offset = domain_index * nb
    dom_ids = jnp.arange(domains)[:, None]
    send_right = jnp.sum(jnp.where(dom_ids == (domain_index + 1) % domains, halo_from_left, 0), axis=0) - offset
    send_left = (
        jnp.sum(jnp.where(dom_ids == (domain_index + domains - 1) % domains, halo_from_right, 0), axis=0)
        - offset
    )

    live = (jnp.arange(slot_count) < tile_count[0]).astype(F32)
    row_oh = (tile_rows[:, None] == jnp.arange(nb)[None, :]).astype(F32) * live[:, None]
    col_oh = (tile_cols[:, None] == jnp.arange(ext)[None, :]).astype(F32)
    pair = (row_oh[:, :, None] * col_oh[:, None, :]).reshape(slot_count, nb * ext)
    adj = jnp.einsum("tp,tij->pij", pair, tile_weights.astype(F32), precision=HIGHEST_PRECISION)
    adj = adj.reshape(nb, ext, blk, blk).transpose(0, 2, 1, 3).reshape(nb * blk, ext * blk)
    adj_hi = adj.astype(BF16)
    adj_lo = (adj - adj_hi.astype(F32)).astype(BF16)
    adj2 = jnp.concatenate([adj_hi, adj_lo], axis=0)

    w_a = w_one[0, :width]
    w_b = w_one[0, width:]
    w_2 = w_two[0]
    gain_row = gain[0]

    both = ("dom", "section")

    def linear(d, s):
        return d * sections + s

    def route(src_section, dst_section, shift):
        return [
            (linear(d, src_section), linear((d + shift) % domains, dst_section))
            for d in range(domains)
        ]

    def forward_layer(h, left, right, split=False):
        if split:
            agg2 = jnp.einsum(
                "ij,sjd->sid", adj2[:, margin : margin + nb * blk], h, preferred_element_type=F32
            )
            halo = jnp.concatenate([left, right], axis=1)
            adj_halo = jnp.concatenate([adj2[:, :margin], adj2[:, margin + nb * blk :]], axis=1)
            agg2 = agg2 + jnp.einsum("ij,sjd->sid", adj_halo, halo, preferred_element_type=F32)
        else:
            h_ext = jnp.concatenate([left, h, right], axis=1)
            agg2 = jnp.einsum("ij,sjd->sid", adj2, h_ext, preferred_element_type=F32)
        agg = (agg2[:, : nb * blk] + agg2[:, nb * blk :]).astype(BF16)
        pre = jnp.einsum("sic,ct->sit", h, w_a, preferred_element_type=F32)
        pre = pre + jnp.einsum("sic,ct->sit", agg, w_b, preferred_element_type=F32)
        act = jax.nn.silu(pre).astype(BF16)
        mixed = jnp.einsum("sic,ct->sit", act, w_2, preferred_element_type=F32)
        center = mixed - jnp.mean(mixed, axis=-1, keepdims=True)
        rstd = lax.rsqrt(jnp.mean(center * center, axis=-1, keepdims=True) + EPSILON)
        normed = center * rstd
        out = (h.astype(F32) + normed * gain_row).astype(BF16)
        return out, (h, agg, pre, act, normed, rstd)

    in_blocks = node_input.reshape(samples, nb, blk, width)
    left = lax.ppermute(pick_blocks(in_blocks, send_right, hs), both, route(0, 0, 1))
    right = lax.ppermute(pick_blocks(in_blocks, send_left, hs), both, route(0, 0, -1))
    h = node_input
    res_list = []
    out_list = []
    for tick in range(sections):
        out, res = forward_layer(h, left, right, split=True)
        res_list.append(res)
        out_list.append(out)
        if tick + 1 < sections:
            out_blocks = out.reshape(samples, nb, blk, width)
            h = lax.ppermute(out, both, route(tick, tick + 1, 0))
            left = lax.ppermute(pick_blocks(out_blocks, send_right, hs), both, route(tick, tick + 1, 1))
            right = lax.ppermute(pick_blocks(out_blocks, send_left, hs), both, route(tick, tick + 1, -1))

    g = cotangent
    formed = []
    dpre_list = []
    dout_list = []
    gain_list = []
    for tick in range(sections):
        _, _, pre_t, _, normed_t, rstd_t = res_list[sections - 1 - tick]
        gf = g.astype(F32)
        gain_term = jnp.sum(gf * normed_t, axis=(0, 1))
        dn = gf * gain_row
        dout = (
            rstd_t
            * (
                dn
                - jnp.mean(dn, axis=-1, keepdims=True)
                - normed_t * jnp.mean(dn * normed_t, axis=-1, keepdims=True)
            )
        ).astype(BF16)
        dact = jnp.einsum("sip,vp->siv", dout, w_2, preferred_element_type=F32)
        sig = jax.nn.sigmoid(pre_t)
        dpre = (dact * sig * (1.0 + pre_t * (1.0 - sig))).astype(BF16)
        gnode = gf + jnp.einsum("sip,vp->siv", dpre, w_a, preferred_element_type=F32)
        dagg = jnp.einsum("sip,vp->siv", dpre, w_b, preferred_element_type=F32).astype(BF16)
        spread = jnp.einsum(
            "ij,sid->sjd", adj2, jnp.concatenate([dagg, dagg], axis=1), preferred_element_type=F32
        )
        left_grad = spread[:, :margin].astype(BF16)
        right_grad = spread[:, margin + nb * blk :].astype(BF16)
        own = gnode + spread[:, margin : margin + nb * blk]

        def finish(partial, from_right, from_left):
            blocks = partial.reshape(samples, nb, blk, width)
            blocks = add_blocks(blocks, send_right, hs, from_right)
            blocks = add_blocks(blocks, send_left, hs, from_left)
            return blocks.reshape(samples, node_rows, width).astype(BF16)

        active = sections - 1 - tick
        mine = section_index == active
        if tick + 1 < sections:
            g = finish(
                lax.ppermute(own.astype(BF16), both, route(active, active - 1, 0)),
                lax.ppermute(left_grad, both, route(active, active - 1, -1)),
                lax.ppermute(right_grad, both, route(active, active - 1, 1)),
            )
            formed.append(g)
            g_new = None
        else:
            g_new = finish(
                own,
                lax.ppermute(left_grad, both, route(active, active, -1)),
                lax.ppermute(right_grad, both, route(active, active, 1)),
            )
        dpre_list.append(dpre)
        dout_list.append(dout)
        gain_list.append(gain_term)

    def own_forward(i):
        return lax.select_n(section_index, *[r[i] for r in res_list])

    def own_backward(values):
        return lax.select_n(sections - 1 - section_index, *values)

    h_in, agg, act = own_forward(0), own_forward(1), own_forward(3)
    saved_out = lax.select_n(section_index, *out_list)
    dpre_keep = own_backward(dpre_list)
    dout_keep = own_backward(dout_list)
    gain_keep = own_backward(gain_list)

    norm_factor = 1.0 / math.sqrt(samples * node_rows * domains)
    stacked = jnp.concatenate([h_in, agg], axis=2)
    gw1 = jnp.einsum("via,vid->ad", stacked, dpre_keep, preferred_element_type=F32)
    gw2 = jnp.einsum("via,vid->ad", act, dout_keep, preferred_element_type=F32)
    r1 = gw1.shape[0] // domains
    r2 = gw2.shape[0] // domains
    r3 = gain_keep.shape[0] // domains
    pad_rows = 16
    gain_rows = jnp.pad(gain_keep.reshape(domains, 1, r3), ((0, 0), (0, pad_rows - 1), (0, width - r3)))
    packed = jnp.concatenate(
        [
            gw1.reshape(domains, r1, width),
            gw2.reshape(domains, r2, width),
            gain_rows,
        ],
        axis=1,
    ).astype(BF16)
    packed = packed.reshape(domains * (r1 + r2 + pad_rows), width)
    reduced = halving_reduce_scatter(packed, "dom", domains, domain_index)
    reduced = reduced.astype(F32) * norm_factor
    g1 = reduced[:r1]
    g2 = reduced[r1 : r1 + r2]
    g3 = reduced[r1 + r2, :r3]
    if formed:
        mine_formed = lax.select_n(
            jnp.clip(sections - 2 - section_index, 0, len(formed) - 1), *formed
        )
        back_pairs = [(linear(d, s), linear(d, s + 1)) for d in range(domains) for s in range(sections - 1)]
        g_back = lax.ppermute(mine_formed, both, back_pairs)
        grad_in = jnp.where(section_index == 0, g_new, g_back)
    else:
        grad_in = g_new
    return (
        saved_out[None],
        grad_in[None],
        g1[None],
        g2[None],
        g3[None],
    )


def solution(mesh):
    return jax.shard_map(
        shards,
        mesh=mesh,
        in_specs=(
            P("groups", "dom", None),
            P("groups", "dom", None),
            P("section", None, None),
            P("section", None, None),
            P("section", None),
            P("dom", None, None),
            P("dom"),
            P("dom"),
            P("dom"),
            P(),
            P(),
        ),
        out_specs=(
            P("section", "groups", "dom", None),
            P("section", "groups", "dom", None),
            P("section", "dom", "groups"),
            P("section", "dom", "groups"),
            P("section", ("groups", "dom")),
        ),
        check_vma=False,
    )
```

```python
import math

import jax
import jax.numpy as jnp
from jax import lax
from jax.sharding import PartitionSpec as P

EPSILON = 1e-05
HIGHEST_PRECISION = lax.Precision.HIGHEST
F32 = jnp.float32
BF16 = jnp.bfloat16


def pick_blocks(blocks, index, count):
    parts = [lax.dynamic_index_in_dim(blocks, index[i], axis=1, keepdims=False) for i in range(count)]
    return jnp.concatenate(parts, axis=1)


def add_blocks(blocks, index, count, values):
    samples, nb, blk, width = blocks.shape
    values = values.reshape(samples, count, blk, width).astype(F32)
    for i in range(count):
        hit = (jnp.arange(nb) == index[i])[None, :, None, None]
        blocks = blocks + jnp.where(hit, values[:, i][:, None], 0.0)
    return blocks


def halving_reduce_scatter(x, axis, devices, index):
    if devices & (devices - 1):
        return lax.psum_scatter(x, axis, scatter_dimension=0, tiled=True)
    rows = x.shape[0] // devices
    cur = x.reshape(devices, rows, x.shape[1]).astype(F32)
    dist = 1
    while dist < devices:
        cur = cur.reshape(cur.shape[0] // 2, 2, rows, x.shape[1])
        bit = (index // dist) % 2
        low, high = cur[:, 0], cur[:, 1]
        keep = jnp.where(bit == 0, low, high)
        send = jnp.where(bit == 0, high, low).astype(x.dtype)
        pairs = [(i, i ^ dist) for i in range(devices)]
        recv = lax.ppermute(send, axis, pairs)
        cur = keep + recv.astype(F32)
        dist *= 2
    return cur[0]


def shards(
    node_input,
    cotangent,
    w_one,
    w_two,
    gain,
    tile_weights,
    tile_rows,
    tile_cols,
    tile_count,
    halo_from_left,
    halo_from_right,
):
    sections = lax.axis_size("section")
    section_index = lax.axis_index("section")
    domains = lax.axis_size("dom")
    domain_index = lax.axis_index("dom")
    samples, node_rows, width = node_input.shape
    slot_count, blk, _ = tile_weights.shape
    nb = node_rows // blk
    hs = halo_from_left.shape[1]
    ext = nb + 2 * hs
    margin = hs * blk
    offset = domain_index * nb
    dom_ids = jnp.arange(domains)[:, None]
    send_right = jnp.sum(jnp.where(dom_ids == (domain_index + 1) % domains, halo_from_left, 0), axis=0) - offset
    send_left = (
        jnp.sum(jnp.where(dom_ids == (domain_index + domains - 1) % domains, halo_from_right, 0), axis=0)
        - offset
    )

    live = (jnp.arange(slot_count) < tile_count[0]).astype(F32)
    row_oh = (tile_rows[:, None] == jnp.arange(nb)[None, :]).astype(F32) * live[:, None]
    col_oh = (tile_cols[:, None] == jnp.arange(ext)[None, :]).astype(F32)
    pair = (row_oh[:, :, None] * col_oh[:, None, :]).reshape(slot_count, nb * ext)
    adj = jnp.einsum("tp,tij->pij", pair, tile_weights.astype(F32), precision=HIGHEST_PRECISION)
    adj = adj.reshape(nb, ext, blk, blk).transpose(0, 2, 1, 3).reshape(nb * blk, ext * blk)
    adj2 = adj.astype(BF16)

    w_a = w_one[0, :width]
    w_b = w_one[0, width:]
    w_2 = w_two[0]
    gain_row = gain[0]

    both = ("dom", "section")

    def linear(d, s):
        return d * sections + s

    def route(src_section, dst_section, shift):
        return [
            (linear(d, src_section), linear((d + shift) % domains, dst_section))
            for d in range(domains)
        ]

    def forward_layer(h, left, right, split=False):
        if split:
            agg2 = jnp.einsum(
                "ij,sjd->sid", adj2[:, margin : margin + nb * blk], h, preferred_element_type=F32
            )
            halo = jnp.concatenate([left, right], axis=1)
            adj_halo = jnp.concatenate([adj2[:, :margin], adj2[:, margin + nb * blk :]], axis=1)
            agg2 = agg2 + jnp.einsum("ij,sjd->sid", adj_halo, halo, preferred_element_type=F32)
        else:
            h_ext = jnp.concatenate([left, h, right], axis=1)
            agg2 = jnp.einsum("ij,sjd->sid", adj2, h_ext, preferred_element_type=F32)
        agg = agg2.astype(BF16)
        pre = jnp.einsum("sic,ct->sit", h, w_a, preferred_element_type=F32)
        pre = pre + jnp.einsum("sic,ct->sit", agg, w_b, preferred_element_type=F32)
        act = jax.nn.silu(pre).astype(BF16)
        mixed = jnp.einsum("sic,ct->sit", act, w_2, preferred_element_type=F32)
        center = mixed - jnp.mean(mixed, axis=-1, keepdims=True)
        rstd = lax.rsqrt(jnp.mean(center * center, axis=-1, keepdims=True) + EPSILON)
        normed = center * rstd
        out = (h.astype(F32) + normed * gain_row).astype(BF16)
        return out, (h, agg, pre, act, normed, rstd)

    in_blocks = node_input.reshape(samples, nb, blk, width)
    left = lax.ppermute(pick_blocks(in_blocks, send_right, hs), both, route(0, 0, 1))
    right = lax.ppermute(pick_blocks(in_blocks, send_left, hs), both, route(0, 0, -1))
    h = node_input
    res_list = []
    out_list = []
    for tick in range(sections):
        out, res = forward_layer(h, left, right, split=tick == 0)
        res_list.append(res)
        out_list.append(out)
        if tick + 1 < sections:
            out_blocks = out.reshape(samples, nb, blk, width)
            h = lax.ppermute(out, both, route(tick, tick + 1, 0))
            left = lax.ppermute(pick_blocks(out_blocks, send_right, hs), both, route(tick, tick + 1, 1))
            right = lax.ppermute(pick_blocks(out_blocks, send_left, hs), both, route(tick, tick + 1, -1))

    g = cotangent
    formed = []
    dpre_list = []
    dout_list = []
    gain_list = []
    for tick in range(sections):
        _, _, pre_t, _, normed_t, rstd_t = res_list[sections - 1 - tick]
        gf = g.astype(F32)
        gain_term = jnp.sum(gf * normed_t, axis=(0, 1))
        dn = gf * gain_row
        dout = (
            rstd_t
            * (
                dn
                - jnp.mean(dn, axis=-1, keepdims=True)
                - normed_t * jnp.mean(dn * normed_t, axis=-1, keepdims=True)
            )
        ).astype(BF16)
        dact = jnp.einsum("sip,vp->siv", dout, w_2, preferred_element_type=F32)
        sig = jax.nn.sigmoid(pre_t)
        dpre = (dact * sig * (1.0 + pre_t * (1.0 - sig))).astype(BF16)
        gnode = gf + jnp.einsum("sip,vp->siv", dpre, w_a, preferred_element_type=F32)
        dagg = jnp.einsum("sip,vp->siv", dpre, w_b, preferred_element_type=F32).astype(BF16)
        spread = jnp.einsum(
            "ij,sid->sjd", adj2, dagg, preferred_element_type=F32
        )
        left_grad = spread[:, :margin].astype(BF16)
        right_grad = spread[:, margin + nb * blk :].astype(BF16)
        own = gnode + spread[:, margin : margin + nb * blk]

        def finish(partial, from_right, from_left):
            blocks = partial.reshape(samples, nb, blk, width)
            blocks = add_blocks(blocks, send_right, hs, from_right)
            blocks = add_blocks(blocks, send_left, hs, from_left)
            return blocks.reshape(samples, node_rows, width).astype(BF16)

        active = sections - 1 - tick
        mine = section_index == active
        if tick + 1 < sections:
            g = finish(
                lax.ppermute(own.astype(BF16), both, route(active, active - 1, 0)),
                lax.ppermute(left_grad, both, route(active, active - 1, -1)),
                lax.ppermute(right_grad, both, route(active, active - 1, 1)),
            )
            formed.append(g)
            g_new = None
        else:
            g_new = finish(
                own,
                lax.ppermute(left_grad, both, route(active, active, -1)),
                lax.ppermute(right_grad, both, route(active, active, 1)),
            )
        dpre_list.append(dpre)
        dout_list.append(dout)
        gain_list.append(gain_term)

    def own_forward(i):
        return lax.select_n(section_index, *[r[i] for r in res_list])

    def own_backward(values):
        return lax.select_n(sections - 1 - section_index, *values)

    h_in, agg, act = own_forward(0), own_forward(1), own_forward(3)
    saved_out = lax.select_n(section_index, *out_list)
    dpre_keep = own_backward(dpre_list)
    dout_keep = own_backward(dout_list)
    gain_keep = own_backward(gain_list)

    norm_factor = 1.0 / math.sqrt(samples * node_rows * domains)
    stacked = jnp.concatenate([h_in, agg], axis=2)
    gw1 = jnp.einsum("via,vid->ad", stacked, dpre_keep, preferred_element_type=F32)
    gw2 = jnp.einsum("via,vid->ad", act, dout_keep, preferred_element_type=F32)
    r1 = gw1.shape[0] // domains
    r2 = gw2.shape[0] // domains
    r3 = gain_keep.shape[0] // domains
    pad_rows = 16
    gain_rows = jnp.pad(gain_keep.reshape(domains, 1, r3), ((0, 0), (0, pad_rows - 1), (0, width - r3)))
    packed = jnp.concatenate(
        [
            gw1.reshape(domains, r1, width),
            gw2.reshape(domains, r2, width),
            gain_rows,
        ],
        axis=1,
    ).astype(BF16)
    packed = packed.reshape(domains * (r1 + r2 + pad_rows), width)
    reduced = halving_reduce_scatter(packed, "dom", domains, domain_index)
    reduced = reduced.astype(F32) * norm_factor
    g1 = reduced[:r1]
    g2 = reduced[r1 : r1 + r2]
    g3 = reduced[r1 + r2, :r3]
    if formed:
        mine_formed = lax.select_n(
            jnp.clip(sections - 2 - section_index, 0, len(formed) - 1), *formed
        )
        back_pairs = [(linear(d, s), linear(d, s + 1)) for d in range(domains) for s in range(sections - 1)]
        g_back = lax.ppermute(mine_formed, both, back_pairs)
        grad_in = jnp.where(section_index == 0, g_new, g_back)
    else:
        grad_in = g_new
    return (
        saved_out[None],
        grad_in[None],
        g1[None],
        g2[None],
        g3[None],
    )


def solution(mesh):
    return jax.shard_map(
        shards,
        mesh=mesh,
        in_specs=(
            P("groups", "dom", None),
            P("groups", "dom", None),
            P("section", None, None),
            P("section", None, None),
            P("section", None),
            P("dom", None, None),
            P("dom"),
            P("dom"),
            P("dom"),
            P(),
            P(),
        ),
        out_specs=(
            P("section", "groups", "dom", None),
            P("section", "groups", "dom", None),
            P("section", "dom", "groups"),
            P("section", "dom", "groups"),
            P("section", ("groups", "dom")),
        ),
        check_vma=False,
    )
```
